128 devices in a mesh: seq: 32 (over x, z, core), tp: 4 (over y).
Axes of the slice: x: 4, y: 4, z: 4, core: 2. Of those that a mesh axis runs over, the one named last changes fastest.
Arguments:
- x_long: bfloat16 [16384, 4096], P('seq', 'tp'), may hold values from -6 to 6
- bc_long: bfloat16 [16384, 2, 512], P('seq', None, 'tp'), may hold values from -6 to 6
- z_long: bfloat16 [16384, 4096], P('seq', 'tp'), may hold values from -6 to 6
- dt_long: bfloat16 [64, 16384], P('tp', 'seq'), may hold values from -2.5 to 13
- x_short: bfloat16 [64, 16, 4096], P('seq', None, 'tp'), may hold values from -6 to 6
- bc_short: bfloat16 [64, 16, 2, 512], P('seq', None, None, 'tp'), may hold values from -6 to 6
- z_short: bfloat16 [64, 16, 4096], P('seq', None, 'tp'), may hold values from -6 to 6
- dt_short: bfloat16 [64, 64, 16], P('tp', 'seq'), may hold values from -3 to 3
- lengths: int32 [64], P('seq'), may hold values from 1 to 16, as said below
- conv_x: float32 [4, 4096], P(None, 'tp'), may hold values from -3 to 3
- conv_bc: float32 [4, 2, 512], P(None, None, 'tp'), may hold values from -3 to 3
- conv_bias_x: float32 [4096], P('tp'), may hold values from -0.5 to 0.5
- conv_bias_bc: float32 [2, 512], P(None, 'tp'), may hold values from -0.5 to 0.5
- dt_bias: float32 [64], P('tp'), may hold values from -9.5 to -1.5
- a_log: float32 [64], P('tp'), may hold values from -1.2 to -0.5
- d_skip: float32 [64], P('tp'), may hold values from 0.5 to 1.5
- norm_gain: float32 [4096], P('tp'), may hold values from 0.1 to 1.9
- out_weight: bfloat16 [4096, 4096], P('tp'), may hold values from -0.09375 to 0.09375
- final_gain: float32 [4096], replicated, may hold values from 0.1 to 1.9
- head_weight: bfloat16 [131072, 4096], P(('seq', 'tp')), may hold values from -0.25 to 0.25
Outputs:
- hidden_long: bfloat16 [16384, 4096], P('seq', 'tp')
- hidden_short: bfloat16 [64, 16, 4096], P('seq', None, 'tp')
- block_states: float32 [32, 64, 64, 128], P('seq', 'tp')
- short_states: float32 [64, 64, 64, 128], P('seq', 'tp')
- tails_x: bfloat16 [64, 3, 4096], P('seq', None, 'tp')
- tails_bc: bfloat16 [64, 3, 2, 512], P('seq', None, None, 'tp')
- last_norm: bfloat16 [65, 4096], replicated
- top_logit: float32 [65], replicated
The draws below stay inside these ranges and needn't reach their ends.
Inputs may be any that keep to these rules, and one draw needn't show every extreme that they name: Request r's real tokens are at positions 0 to lengths[r] - 1; some request has 16.
All inputs are finite; a program needn't handle non-finite values.
Results may differ from the reference program's by a relative error of at most 0.014.
Values may be sent and summed in bfloat16 or wider, within the bound.
No kernel may reach another device: no remote copies, remote signals or barrier semaphores. Data moves between devices by JAX's collectives and lax.ppermute only.
A program may use at most 128 MiB of HBM per device.

```python
import jax
import jax.numpy as jnp
from jax import lax

D = 4096
HEAD_SHARE = 64
HEADDIM = 64
GROUPS = 4
STATE = 128
KCONV = 4
BLOCK = 256
SLEN = 16
TOK_DEV = 512
INNER = 4096
GN = 512
PROMPT_POSITIONS = 16384
REQ = 64
VOCAB = 131072
N_TP = 4


def draw_dt_bias(key, part):
    key_pick, key_slow, key_fast = jax.random.split(key, 3)
    slow_share = 0.6
    is_slow = jax.random.uniform(key_pick, (HEAD_SHARE,)) < slow_share
    slow_bias = jax.random.uniform(key_slow, (HEAD_SHARE,), jnp.float32, -9.5, -8.5)
    fast_bias = jax.random.uniform(key_fast, (HEAD_SHARE,), jnp.float32, -2.5, -1.5)
    return jnp.where(is_slow, slow_bias, fast_bias)


def draw_dt_long(key, part):
    random_key_base, random_key_depth, random_key_spike, random_key_length = jax.random.split(key, 4)
    base_portion_rows = jnp.clip(0.3 * jax.random.normal(random_key_base, (HEAD_SHARE, PROMPT_POSITIONS), jnp.float32), -1.5, 1.5)
    device_level = jax.random.uniform(random_key_depth, (HEAD_SHARE, PROMPT_POSITIONS // TOK_DEV), jnp.float32, -0.7, 0.7)
    block_depth = jnp.repeat(device_level, TOK_DEV, axis=1)
    spike_mask = jax.random.uniform(random_key_spike, (HEAD_SHARE, PROMPT_POSITIONS)) < 4.0 / PROMPT_POSITIONS
    spike_length = jax.random.uniform(random_key_length, (HEAD_SHARE, PROMPT_POSITIONS), jnp.float32, 9.0, 10.5)
    return (base_portion_rows + block_depth + jnp.where(spike_mask, spike_length, 0.0)).astype(jnp.bfloat16)


def draw_lengths(key, part):
    random_key_base, key_full = jax.random.split(key, 2)
    base_lengths = jax.random.randint(random_key_base, (REQ,), 1, SLEN + 1)
    full_slot = jax.random.randint(key_full, (), 0, REQ)
    return jnp.where(jnp.arange(REQ) == full_slot, SLEN, base_lengths).astype(jnp.int32)


def block_scale(key, dims, cuts, least, top_value):
    factor_of, own = 1.0, jax.random.fold_in(key, 6)
    for position, blocks in cuts:
        heights = jnp.exp(jax.random.uniform(jax.random.fold_in(own, position), (blocks,), jnp.float32, least / len(cuts), top_value / len(cuts)))
        factor_of = factor_of * jnp.repeat(heights, dims[position] // blocks).reshape([-1 if axis == position else 1 for axis in range(len(dims))])
    return factor_of


def gaussian(stream_key, extent, width, reach, cuts=(), dtype=jnp.bfloat16):
    factor_of = block_scale(stream_key, extent, cuts, -0.22, 0.18) if cuts else 1.0
    result = jax.random.normal(stream_key, extent, jnp.float32) * width * factor_of
    return jnp.minimum(jnp.maximum(result, -reach), reach).astype(dtype)


def setup_inputs(seed: int = 0) -> dict:
    keys = jax.random.split(jax.random.key(seed), 21)
    return {
        "x_long": gaussian(keys[0], (PROMPT_POSITIONS, INNER), 1.0, 6.0, ((0, 32), (1, 4))),
        "bc_long": gaussian(keys[1], (PROMPT_POSITIONS, 2, GN), 1.0, 6.0, ((0, 32), (2, 4))),
        "z_long": gaussian(keys[2], (PROMPT_POSITIONS, INNER), 1.0, 6.0, ((0, 32), (1, 4))),
        "dt_long": draw_dt_long(jax.random.fold_in(keys[20], 71), 0),
        "x_short": gaussian(keys[4], (REQ, SLEN, INNER), 1.0, 6.0, ((0, 32), (2, 4))),
        "bc_short": gaussian(keys[5], (REQ, SLEN, 2, GN), 1.0, 6.0, ((0, 32), (3, 4))),
        "z_short": gaussian(keys[6], (REQ, SLEN, INNER), 1.0, 6.0, ((0, 32), (2, 4))),
        "dt_short": gaussian(keys[7], (HEAD_SHARE, REQ, SLEN), 0.5, 3.0, ((0, 4), (1, 32))),
        "lengths": draw_lengths(jax.random.fold_in(keys[20], 71), 0),
        "conv_x": gaussian(keys[9], (KCONV, INNER), KCONV ** -0.5, 3.0, ((1, 4),), jnp.float32),
        "conv_bc": gaussian(keys[10], (KCONV, 2, GN), KCONV ** -0.5, 3.0, ((2, 4),), jnp.float32),
        "conv_bias_x": jnp.clip(jax.random.uniform(keys[11], (INNER,), jnp.float32, -0.5, 0.5) * block_scale(keys[11], (INNER,), ((0, 4),), -0.4, 0.0), -0.5, 0.5),
        "conv_bias_bc": jnp.clip(jax.random.uniform(keys[12], (2, GN), jnp.float32, -0.5, 0.5) * block_scale(keys[12], (2, GN), ((1, 4),), -0.4, 0.0), -0.5, 0.5),
        "dt_bias": draw_dt_bias(jax.random.fold_in(keys[20], 71), 0),
        "a_log": jnp.clip(-1.2 + 0.70000005 * jax.random.uniform(keys[14], (HEAD_SHARE,), jnp.float32) ** block_scale(keys[14], (HEAD_SHARE,), ((0, 4),), -0.2, 0.2), -1.2, -0.5),
        "d_skip": jnp.clip(0.5 + 1.0 * jax.random.uniform(keys[15], (HEAD_SHARE,), jnp.float32) ** block_scale(keys[15], (HEAD_SHARE,), ((0, 4),), -0.2, 0.2), 0.5, 1.5),
        "norm_gain": jnp.clip(1.0 + 0.18 * jax.random.normal(keys[16], (INNER,), jnp.float32), 0.1, 1.9),
        "out_weight": gaussian(keys[17], (INNER, D), INNER ** -0.5, 0.09375, ((0, 4),)),
        "final_gain": jnp.clip(1.0 + 0.18 * jax.random.normal(keys[18], (D,), jnp.float32), 0.1, 1.9),
        "head_weight": gaussian(keys[19], (VOCAB, D), (D // 9) ** -0.5, 0.25, ((0, 128),)),
    }


def conv_act(inputs, weight, shift_bias):
    span_len = inputs.shape[0]
    padded = jnp.concatenate([jnp.zeros((KCONV - 1,) + inputs.shape[1:], jnp.float32), inputs.astype(jnp.float32)], 0)
    running_sum = shift_bias + 0.0 * padded[:span_len]
    for offset in range(KCONV):
        running_sum = running_sum + weight[offset] * padded[offset:offset + span_len]
    return jax.nn.silu(running_sum).astype(jnp.bfloat16)

def expand(portion):
    shaped = portion.reshape(portion.shape[:-1] + (portion.shape[-1] // STATE, STATE))
    return jnp.repeat(shaped, HEAD_SHARE // GROUPS, axis=-2)

def ssd_block(x_block, b_block, c_block, dt_block, decay_rate, state_in):
    step_log = dt_block * decay_rate[:, None]
    cumulative = jnp.cumsum(step_log, axis=1)
    span_len = x_block.shape[0]
    positions = jnp.arange(span_len)
    causal = (positions[:, None] >= positions[None, :])[None]
    log_gap = jnp.where(causal, cumulative[:, :, None] - cumulative[:, None, :], 0.0)
    decay_table = jnp.where(causal, jnp.exp(log_gap), 0.0)
    scores = jnp.einsum('thn,shn->hts', c_block.astype(jnp.float32), b_block.astype(jnp.float32))
    weights = (scores * decay_table * dt_block[:, None, :]).astype(jnp.bfloat16)
    y_intra = jnp.einsum('hts,shp->thp', weights.astype(jnp.float32), x_block.astype(jnp.float32))
    y_state = jnp.exp(cumulative).T[:, :, None] * jnp.einsum('thn,hpn->thp', c_block.astype(jnp.float32), state_in, precision=lax.Precision.HIGHEST)
    to_end = jnp.exp(cumulative[:, -1:] - cumulative) * dt_block
    scaled = (x_block.astype(jnp.float32) * to_end.T[:, :, None]).astype(jnp.bfloat16)
    next_state = jnp.exp(cumulative[:, -1])[:, None, None] * state_in + jnp.einsum('shp,shn->hpn', scaled.astype(jnp.float32), b_block.astype(jnp.float32))
    return (y_intra + y_state, next_state)

def gate_norm(values, gating, scales):
    gated_rows = values * jax.nn.silu(gating.astype(jnp.float32))
    size_group = HEAD_SHARE // GROUPS * HEADDIM
    shaped = gated_rows.reshape(gated_rows.shape[0], -1, size_group)
    inv_rms = lax.rsqrt(lax.optimization_barrier(jnp.mean(shaped * shaped, axis=-1, keepdims=True)) + 1e-05)
    return ((shaped * inv_rms).reshape(gated_rows.shape) * scales).astype(jnp.bfloat16)

def project(normed, out_weight):
    width_piece = INNER // N_TP
    running_sum = jnp.zeros((normed.shape[0], D), jnp.float32)
    for index in range(N_TP):
        partial_value = jnp.dot(normed[:, index * width_piece:(index + 1) * width_piece], out_weight[index * width_piece:(index + 1) * width_piece], preferred_element_type=jnp.float32)
        partial_value = lax.optimization_barrier(partial_value.astype(jnp.bfloat16))
        running_sum = running_sum + partial_value.astype(jnp.float32)
    return running_sum.astype(jnp.bfloat16)

def reference(x_long, bc_long, z_long, dt_long, x_short, bc_short, z_short, dt_short, lengths, conv_x, conv_bc, conv_bias_x, conv_bias_bc, dt_bias, a_log, d_skip, norm_gain, out_weight, final_gain, head_weight):
    decay_rate = -jnp.exp(a_log)
    x_act = conv_act(x_long, conv_x, conv_bias_x)
    bc_act = conv_act(bc_long, conv_bc, conv_bias_bc)
    dt_full = jax.nn.softplus(dt_long.astype(jnp.float32) + dt_bias[:, None])
    block_count = PROMPT_POSITIONS // BLOCK
    x_blocks = x_act.reshape(block_count, BLOCK, HEAD_SHARE, HEADDIM)
    b_blocks = expand(bc_act[:, 0]).reshape(block_count, BLOCK, HEAD_SHARE, STATE)
    c_blocks = expand(bc_act[:, 1]).reshape(block_count, BLOCK, HEAD_SHARE, STATE)
    dt_blocks = dt_full.reshape(HEAD_SHARE, block_count, BLOCK).transpose(1, 0, 2)

    def advance(carry_state, inputs):
        y_block, next_state = ssd_block(inputs[0], inputs[1], inputs[2], inputs[3], decay_rate, carry_state)
        return (next_state, (y_block, next_state))
    start_state = jnp.zeros((HEAD_SHARE, HEADDIM, STATE), jnp.float32)
    unused, (y_blocks, states) = lax.scan(advance, start_state, (x_blocks, b_blocks, c_blocks, dt_blocks))
    y_long = y_blocks.reshape(PROMPT_POSITIONS, HEAD_SHARE, HEADDIM) + d_skip[None, :, None] * x_act.reshape(PROMPT_POSITIONS, HEAD_SHARE, HEADDIM).astype(jnp.float32)
    per_device = TOK_DEV // BLOCK
    block_states = states[per_device - 1::per_device]
    hidden_long = project(gate_norm(y_long.reshape(PROMPT_POSITIONS, INNER), z_long, norm_gain), out_weight)
    is_valid = jnp.arange(SLEN)[None, :] < lengths[:, None]
    x_sact = jax.vmap(lambda item: conv_act(item, conv_x, conv_bias_x))(x_short)
    bc_sact = jax.vmap(lambda item: conv_act(item, conv_bc, conv_bias_bc))(bc_short)
    dt_sfull = jax.nn.softplus(dt_short.astype(jnp.float32) + dt_bias[:, None, None]) * is_valid[None].astype(jnp.float32)
    dt_sfull = dt_sfull.transpose(1, 0, 2)

    def per_request(x_req, bc_req, dt_req):
        return ssd_block(x_req.reshape(SLEN, HEAD_SHARE, HEADDIM), expand(bc_req[:, 0]), expand(bc_req[:, 1]), dt_req, decay_rate, start_state)
    y_sblocks, short_states = jax.vmap(per_request)(x_sact, bc_sact, dt_sfull)
    y_short = y_sblocks + d_skip[None, None, :, None] * x_sact.reshape(REQ, SLEN, HEAD_SHARE, HEADDIM).astype(jnp.float32)
    normed_short = gate_norm(y_short.reshape(REQ * SLEN, INNER), z_short.reshape(REQ * SLEN, INNER), norm_gain)
    hidden_short = project(normed_short, out_weight).reshape(REQ, SLEN, D) * is_valid[:, :, None].astype(jnp.bfloat16)
    tail_pick = (jnp.arange(SLEN)[None, None, :] == (lengths[:, None] - (KCONV - 1) + jnp.arange(KCONV - 1)[None, :])[:, :, None]).astype(jnp.float32)
    tails_x = jnp.einsum('rks,rsc->rkc', tail_pick, x_short.astype(jnp.float32), precision=lax.Precision.HIGHEST).astype(jnp.bfloat16)
    tails_bc = jnp.einsum('rks,rsbc->rkbc', tail_pick, bc_short.astype(jnp.float32), precision=lax.Precision.HIGHEST).astype(jnp.bfloat16)
    last_pick = (jnp.arange(SLEN)[None, :] == lengths[:, None] - 1).astype(jnp.float32)
    short_rows = jnp.einsum('rs,rsd->rd', last_pick, hidden_short.astype(jnp.float32), precision=lax.Precision.HIGHEST)
    row_block = jnp.concatenate([hidden_long[PROMPT_POSITIONS - 1:].astype(jnp.float32), short_rows], 0)
    last_norm = (row_block * lax.rsqrt(lax.optimization_barrier(jnp.mean(row_block * row_block, axis=-1, keepdims=True)) + 1e-05) * final_gain).astype(jnp.bfloat16)
    logits = lax.dot_general(last_norm, head_weight, (((1,), (1,)), ((), ())), preferred_element_type=jnp.float32)
    top_logit = lax.optimization_barrier(jnp.max(logits, axis=1))
    return (hidden_long, hidden_short, block_states, short_states, tails_x, tails_bc, last_norm, top_logit)
```

```python
import jax
import jax.numpy as jnp
from jax import lax
from jax.sharding import PartitionSpec as P

D = 4096
HEAD_SHARE = 64
HEADDIM = 64
GROUPS = 4
STATE = 128
KCONV = 4
BLOCK = 256
SLEN = 16


def passed_along(block, axis, distance):
    devices = range(lax.axis_size(axis))
    route = [(i - distance, i) for i in devices if i - distance in devices]
    return lax.ppermute(block, axis, route)


def swapped(block, axis, distance):
    devices = range(lax.axis_size(axis))
    return lax.ppermute(block, axis, [(i, i ^ distance) for i in devices])


def gather_all(block, axis, dim):
    count = lax.axis_size(axis)
    index = lax.axis_index(axis)
    distance = 1
    while distance < count:
        other = swapped(block, axis, distance)
        low = (index // distance) % 2 == 0
        block = jnp.where(
            low, jnp.concatenate([block, other], dim), jnp.concatenate([other, block], dim)
        )
        distance *= 2
    return block


def max_all(block, axis):
    distance = 1
    while distance < lax.axis_size(axis):
        block = jnp.maximum(block, swapped(block, axis, distance))
        distance *= 2
    return block


def carry_scan(total_log, local_state, axis):
    sent = local_state.astype(jnp.bfloat16)
    log_one, state_one = passed_along((total_log, sent), axis, 1)
    log_two, state_two = passed_along((total_log, sent), axis, 2)
    seg_log = log_one + log_two
    seg_state = jnp.exp(log_one)[:, None, None] * state_two.astype(jnp.float32) + state_one.astype(
        jnp.float32
    )
    distance = 2
    while distance < lax.axis_size(axis):
        got_log, got_state = passed_along(
            (seg_log, seg_state.astype(jnp.bfloat16)), axis, distance
        )
        seg_state = jnp.exp(seg_log)[:, None, None] * got_state.astype(jnp.float32) + seg_state
        seg_log = seg_log + got_log
        distance *= 2
    return seg_state


def conv_act(padded, weight, shift_bias, span_len):
    running_sum = shift_bias + 0.0 * padded[:span_len].astype(jnp.float32)
    for offset in range(weight.shape[0]):
        running_sum = running_sum + weight[offset] * padded[offset : offset + span_len].astype(
            jnp.float32
        )
    return jax.nn.silu(running_sum).astype(jnp.bfloat16)


def expand(portion):
    shaped = portion.reshape(portion.shape[:-1] + (portion.shape[-1] // STATE, STATE))
    return jnp.repeat(shaped, HEAD_SHARE // GROUPS, axis=-2)


def ssd_block(x_block, b_block, c_block, dt_block, decay_rate, state_in):
    step_log = dt_block * decay_rate[:, None]
    cumulative = jnp.cumsum(step_log, axis=1)
    span_len = x_block.shape[0]
    positions = jnp.arange(span_len)
    causal = (positions[:, None] >= positions[None, :])[None]
    log_gap = jnp.where(causal, cumulative[:, :, None] - cumulative[:, None, :], 0.0)
    decay_table = jnp.where(causal, jnp.exp(log_gap), 0.0)
    scores = jnp.einsum("thn,shn->hts", c_block, b_block, preferred_element_type=jnp.float32)
    weights = (scores * decay_table * dt_block[:, None, :]).astype(jnp.bfloat16)
    y_intra = jnp.einsum("hts,shp->thp", weights, x_block, preferred_element_type=jnp.float32)
    y_state = jnp.exp(cumulative).T[:, :, None] * jnp.einsum(
        "thn,hpn->thp", c_block.astype(jnp.float32), state_in, precision=lax.Precision.HIGHEST
    )
    to_end = jnp.exp(cumulative[:, -1:] - cumulative) * dt_block
    scaled = (x_block.astype(jnp.float32) * to_end.T[:, :, None]).astype(jnp.bfloat16)
    next_state = jnp.exp(cumulative[:, -1])[:, None, None] * state_in + jnp.einsum(
        "shp,shn->hpn", scaled, b_block, preferred_element_type=jnp.float32
    )
    return (y_intra + y_state, next_state)


def gate_norm(values, gating, scales):
    gated_rows = values * jax.nn.silu(gating.astype(jnp.float32))
    size_group = HEAD_SHARE // GROUPS * HEADDIM
    shaped = gated_rows.reshape(gated_rows.shape[0], -1, size_group)
    inv_rms = lax.rsqrt(jnp.mean(shaped * shaped, axis=-1, keepdims=True) + 1e-05)
    return ((shaped * inv_rms).reshape(gated_rows.shape) * scales).astype(jnp.bfloat16)


def local(
    x_long,
    bc_long,
    z_long,
    dt_long,
    x_short,
    bc_short,
    z_short,
    dt_short,
    lengths,
    conv_x,
    conv_bc,
    conv_bias_x,
    conv_bias_bc,
    dt_bias,
    a_log,
    d_skip,
    norm_gain,
    out_weight,
    final_gain,
    head_weight,
):
    tok_rows, inner_cols = x_long.shape
    head_count = dt_long.shape[0]
    req_count = lengths.shape[0]
    rim_rows = KCONV - 1
    decay_rate = -jnp.exp(a_log)
    rim_x, rim_bc = passed_along(
        (x_long[tok_rows - rim_rows :], bc_long[tok_rows - rim_rows :]), "seq", 1
    )
    x_act = conv_act(jnp.concatenate([rim_x, x_long], 0), conv_x, conv_bias_x, tok_rows)
    bc_act = conv_act(jnp.concatenate([rim_bc, bc_long], 0), conv_bc, conv_bias_bc, tok_rows)
    dt_full = jax.nn.softplus(dt_long.astype(jnp.float32) + dt_bias[:, None])
    block_count = tok_rows // BLOCK
    x_blocks = x_act.reshape(block_count, BLOCK, head_count, HEADDIM)
    b_blocks = expand(bc_act[:, 0]).reshape(block_count, BLOCK, head_count, STATE)
    c_all = expand(bc_act[:, 1])
    c_blocks = c_all.reshape(block_count, BLOCK, head_count, STATE)
    dt_blocks = dt_full.reshape(head_count, block_count, BLOCK).transpose(1, 0, 2)

    start_state = jnp.zeros((head_count, HEADDIM, STATE), jnp.float32)
    local_state = start_state
    y_parts = []
    for index in range(block_count):
        y_block, local_state = ssd_block(
            x_blocks[index], b_blocks[index], c_blocks[index], dt_blocks[index], decay_rate, local_state
        )
        y_parts.append(y_block)
    y_blocks = jnp.stack(y_parts)
    cum_device = jnp.cumsum(dt_full * decay_rate[:, None], axis=1)
    total_log = cum_device[:, -1]
    carry_in = carry_scan(total_log, local_state, "seq")
    carried = jnp.exp(cum_device).T[:, :, None] * jnp.einsum(
        "thn,hpn->thp", c_all.astype(jnp.float32), carry_in, precision=lax.Precision.HIGHEST
    )
    y_long = (
        y_blocks.reshape(tok_rows, head_count, HEADDIM)
        + carried
        + d_skip[None, :, None] * x_act.reshape(tok_rows, head_count, HEADDIM).astype(jnp.float32)
    )
    block_states = (jnp.exp(total_log)[:, None, None] * carry_in + local_state)[None]
    normed_long = gate_norm(y_long.reshape(tok_rows, inner_cols), z_long, norm_gain)
    is_valid = jnp.arange(SLEN)[None, :] < lengths[:, None]
    zero_x = jnp.zeros((req_count, rim_rows) + x_short.shape[2:], jnp.bfloat16)
    zero_bc = jnp.zeros((req_count, rim_rows) + bc_short.shape[2:], jnp.bfloat16)
    x_sact = jax.vmap(lambda item: conv_act(item, conv_x, conv_bias_x, SLEN))(
        jnp.concatenate([zero_x, x_short], 1)
    )
    bc_sact = jax.vmap(lambda item: conv_act(item, conv_bc, conv_bias_bc, SLEN))(
        jnp.concatenate([zero_bc, bc_short], 1)
    )
    dt_sfull = jax.nn.softplus(dt_short.astype(jnp.float32) + dt_bias[:, None, None]) * is_valid[
        None
    ].astype(jnp.float32)
    dt_sfull = dt_sfull.transpose(1, 0, 2)

    def per_request(x_req, bc_req, dt_req):
        return ssd_block(
            x_req.reshape(SLEN, head_count, HEADDIM),
            expand(bc_req[:, 0]),
            expand(bc_req[:, 1]),
            dt_req,
            decay_rate,
            start_state,
        )

    y_sblocks, short_states = jax.vmap(per_request)(x_sact, bc_sact, dt_sfull)
    y_short = y_sblocks + d_skip[None, None, :, None] * x_sact.reshape(
        req_count, SLEN, head_count, HEADDIM
    ).astype(jnp.float32)
    normed_short = gate_norm(
        y_short.reshape(req_count * SLEN, inner_cols),
        z_short.reshape(req_count * SLEN, inner_cols),
        norm_gain,
    )
    tail_pick = (
        jnp.arange(SLEN)[None, None, :]
        == (lengths[:, None] - rim_rows + jnp.arange(rim_rows)[None, :])[:, :, None]
    ).astype(jnp.float32)
    tails_x = jnp.einsum(
        "rks,rsc->rkc", tail_pick, x_short.astype(jnp.float32), precision=lax.Precision.HIGHEST
    ).astype(jnp.bfloat16)
    tails_bc = jnp.einsum(
        "rks,rsbc->rkbc", tail_pick, bc_short.astype(jnp.float32), precision=lax.Precision.HIGHEST
    ).astype(jnp.bfloat16)
    all_normed = jnp.concatenate([normed_long, normed_short], 0)
    tp_count = lax.axis_size("tp")
    tp_index = lax.axis_index("tp")
    width = out_weight.shape[1] // tp_count
    total = None
    for step in (2, 1, 3, 0):
        if step >= tp_count:
            continue
        target = (tp_index + step) % tp_count
        piece = lax.dynamic_slice_in_dim(out_weight, target * width, width, 1)
        term = jnp.dot(all_normed, piece, preferred_element_type=jnp.float32).astype(jnp.bfloat16)
        if step:
            term = lax.ppermute(
                term, "tp", [(i, (i + step) % tp_count) for i in range(tp_count)]
            )
        total = term.astype(jnp.float32) if total is None else total + term.astype(jnp.float32)
    hidden = total.astype(jnp.bfloat16)
    hidden_long = hidden[:tok_rows]
    hidden_short = hidden[tok_rows:].reshape(req_count, SLEN, -1) * is_valid[:, :, None].astype(
        jnp.bfloat16
    )
    last_pick = (jnp.arange(SLEN)[None, :] == lengths[:, None] - 1).astype(jnp.float32)
    short_rows = jnp.einsum(
        "rs,rsd->rd", last_pick, hidden_short.astype(jnp.float32), precision=lax.Precision.HIGHEST
    ).astype(jnp.bfloat16)
    packed = jnp.concatenate([short_rows, hidden_long[tok_rows - 1 :]], 0)
    seq_rows = gather_all(packed, "seq", 0)
    full_rows = gather_all(seq_rows, "tp", 1)
    seq_count = lax.axis_size("seq")
    shaped = full_rows.reshape(seq_count, req_count + 1, D)
    long_row = shaped[seq_count - 1, req_count][None]
    short_all = shaped[:, :req_count].reshape(seq_count * req_count, D)
    row_block = jnp.concatenate([long_row, short_all], 0).astype(jnp.float32)
    last_norm = (
        row_block
        * lax.rsqrt(jnp.mean(row_block * row_block, axis=-1, keepdims=True) + 1e-05)
        * final_gain
    ).astype(jnp.bfloat16)
    logits = lax.dot_general(
        last_norm, head_weight, (((1,), (1,)), ((), ())), preferred_element_type=jnp.float32
    )
    top_logit = max_all(max_all(jnp.max(logits, axis=1), "tp"), "seq")
    return (
        hidden_long,
        hidden_short,
        block_states,
        short_states,
        tails_x,
        tails_bc,
        last_norm,
        top_logit,
    )


def solution(mesh):
    in_specs = (
        P("seq", "tp"),
        P("seq", None, "tp"),
        P("seq", "tp"),
        P("tp", "seq"),
        P("seq", None, "tp"),
        P("seq", None, None, "tp"),
        P("seq", None, "tp"),
        P("tp", "seq", None),
        P("seq"),
        P(None, "tp"),
        P(None, None, "tp"),
        P("tp"),
        P(None, "tp"),
        P("tp"),
        P("tp"),
        P("tp"),
        P("tp"),
        P("tp", None),
        P(),
        P(("seq", "tp"), None),
    )
    out_specs = (
        P("seq", "tp"),
        P("seq", None, "tp"),
        P("seq", "tp", None, None),
        P("seq", "tp", None, None),
        P("seq", None, "tp"),
        P("seq", None, None, "tp"),
        P(),
        P(),
    )
    return jax.shard_map(local, mesh=mesh, in_specs=in_specs, out_specs=out_specs, check_vma=False)
```

```python
import jax
import jax.numpy as jnp
from jax import lax
from jax.sharding import PartitionSpec as P

D = 4096
HEAD_SHARE = 64
HEADDIM = 64
GROUPS = 4
STATE = 128
KCONV = 4
BLOCK = 256
SLEN = 16


def passed_along(block, axis, distance):
    devices = range(lax.axis_size(axis))
    route = [(i - distance, i) for i in devices if i - distance in devices]
    return lax.ppermute(block, axis, route)


def swapped(block, axis, distance):
    devices = range(lax.axis_size(axis))
    return lax.ppermute(block, axis, [(i, i ^ distance) for i in devices])


def gather_all(block, axis, dim):
    count = lax.axis_size(axis)
    index = lax.axis_index(axis)
    distance = 1
    while distance < count:
        other = swapped(block, axis, distance)
        low = (index // distance) % 2 == 0
        block = jnp.where(
            low, jnp.concatenate([block, other], dim), jnp.concatenate([other, block], dim)
        )
        distance *= 2
    return block


def max_all(block, axis):
    distance = 1
    while distance < lax.axis_size(axis):
        block = jnp.maximum(block, swapped(block, axis, distance))
        distance *= 2
    return block


def from_last(block, axis):
    count = lax.axis_size(axis)
    index = lax.axis_index(axis)
    source = count - 1
    distance = 1
    while distance < count:
        other = swapped(block, axis, distance)
        keep = (index // distance) % 2 == (source // distance) % 2
        block = jnp.where(keep, block, other)
        distance *= 2
    return block


def tp_rows(rows, out_weight):
    part = jnp.dot(rows, out_weight, preferred_element_type=jnp.float32).astype(jnp.bfloat16)
    count = lax.axis_size("tp")
    index = lax.axis_index("tp")
    got = [part] + [
        lax.ppermute(part, "tp", [(i, (i + step) % count) for i in range(count)])
        for step in range(1, count)
    ]
    stacked = jnp.stack(got)
    total = jnp.zeros(part.shape, jnp.float32)
    for source in range(count):
        pick = lax.dynamic_index_in_dim(stacked, (index - source) % count, 0, keepdims=False)
        total = total + pick.astype(jnp.float32)
    return total.astype(jnp.bfloat16)


def row_norm(rows, final_gain):
    rows = rows.astype(jnp.float32)
    return (
        rows * lax.rsqrt(jnp.mean(rows * rows, axis=-1, keepdims=True) + 1e-05) * final_gain
    ).astype(jnp.bfloat16)


def carry_scan(total_log, local_state, axis):
    sent = local_state.astype(jnp.bfloat16)
    log_one, state_one = passed_along((total_log, sent), axis, 1)
    log_two, state_two = passed_along((total_log, sent), axis, 2)
    seg_log = log_one + log_two
    seg_state = jnp.exp(log_one)[:, None, None] * state_two.astype(jnp.float32) + state_one.astype(
        jnp.float32
    )
    distance = 2
    while distance < lax.axis_size(axis):
        got_log, got_state = passed_along(
            (seg_log, seg_state.astype(jnp.bfloat16)), axis, distance
        )
        seg_state = jnp.exp(seg_log)[:, None, None] * got_state.astype(jnp.float32) + seg_state
        seg_log = seg_log + got_log
        distance *= 2
    return seg_state


def conv_act(padded, weight, shift_bias, span_len):
    running_sum = shift_bias + 0.0 * padded[:span_len].astype(jnp.float32)
    for offset in range(weight.shape[0]):
        running_sum = running_sum + weight[offset] * padded[offset : offset + span_len].astype(
            jnp.float32
        )
    return jax.nn.silu(running_sum).astype(jnp.bfloat16)


def expand(portion):
    shaped = portion.reshape(portion.shape[:-1] + (portion.shape[-1] // STATE, STATE))
    return jnp.repeat(shaped, HEAD_SHARE // GROUPS, axis=-2)


def ssd_block(x_block, b_block, c_block, dt_block, decay_rate, state_in):
    step_log = dt_block * decay_rate[:, None]
    cumulative = jnp.cumsum(step_log, axis=1)
    span_len = x_block.shape[0]
    positions = jnp.arange(span_len)
    causal = (positions[:, None] >= positions[None, :])[None]
    log_gap = jnp.where(causal, cumulative[:, :, None] - cumulative[:, None, :], 0.0)
    decay_table = jnp.where(causal, jnp.exp(log_gap), 0.0)
    scores = jnp.einsum("thn,shn->hts", c_block, b_block, preferred_element_type=jnp.float32)
    weights = (scores * decay_table * dt_block[:, None, :]).astype(jnp.bfloat16)
    y_intra = jnp.einsum("hts,shp->thp", weights, x_block, preferred_element_type=jnp.float32)
    y_state = jnp.exp(cumulative).T[:, :, None] * jnp.einsum(
        "thn,hpn->thp", c_block.astype(jnp.float32), state_in, precision=lax.Precision.HIGHEST
    )
    to_end = jnp.exp(cumulative[:, -1:] - cumulative) * dt_block
    scaled = (x_block.astype(jnp.float32) * to_end.T[:, :, None]).astype(jnp.bfloat16)
    next_state = jnp.exp(cumulative[:, -1])[:, None, None] * state_in + jnp.einsum(
        "shp,shn->hpn", scaled, b_block, preferred_element_type=jnp.float32
    )
    return (y_intra + y_state, next_state)


def gate_norm(values, gating, scales):
    gated_rows = values * jax.nn.silu(gating.astype(jnp.float32))
    size_group = HEAD_SHARE // GROUPS * HEADDIM
    shaped = gated_rows.reshape(gated_rows.shape[0], -1, size_group)
    inv_rms = lax.rsqrt(jnp.mean(shaped * shaped, axis=-1, keepdims=True) + 1e-05)
    return ((shaped * inv_rms).reshape(gated_rows.shape) * scales).astype(jnp.bfloat16)


def local(
    x_long,
    bc_long,
    z_long,
    dt_long,
    x_short,
    bc_short,
    z_short,
    dt_short,
    lengths,
    conv_x,
    conv_bc,
    conv_bias_x,
    conv_bias_bc,
    dt_bias,
    a_log,
    d_skip,
    norm_gain,
    out_weight,
    final_gain,
    head_weight,
):
    tok_rows, inner_cols = x_long.shape
    head_count = dt_long.shape[0]
    req_count = lengths.shape[0]
    rim_rows = KCONV - 1
    decay_rate = -jnp.exp(a_log)
    rim_x, rim_bc = passed_along(
        (x_long[tok_rows - rim_rows :], bc_long[tok_rows - rim_rows :]), "seq", 1
    )
    x_act = conv_act(jnp.concatenate([rim_x, x_long], 0), conv_x, conv_bias_x, tok_rows)
    bc_act = conv_act(jnp.concatenate([rim_bc, bc_long], 0), conv_bc, conv_bias_bc, tok_rows)
    dt_full = jax.nn.softplus(dt_long.astype(jnp.float32) + dt_bias[:, None])
    block_count = tok_rows // BLOCK
    x_blocks = x_act.reshape(block_count, BLOCK, head_count, HEADDIM)
    b_blocks = expand(bc_act[:, 0]).reshape(block_count, BLOCK, head_count, STATE)
    c_all = expand(bc_act[:, 1])
    c_blocks = c_all.reshape(block_count, BLOCK, head_count, STATE)
    dt_blocks = dt_full.reshape(head_count, block_count, BLOCK).transpose(1, 0, 2)

    start_state = jnp.zeros((head_count, HEADDIM, STATE), jnp.float32)
    local_state = start_state
    y_parts = []
    for index in range(block_count):
        y_block, local_state = ssd_block(
            x_blocks[index], b_blocks[index], c_blocks[index], dt_blocks[index], decay_rate, local_state
        )
        y_parts.append(y_block)
    y_blocks = jnp.stack(y_parts)
    cum_device = jnp.cumsum(dt_full * decay_rate[:, None], axis=1)
    total_log = cum_device[:, -1]
    carry_in = carry_scan(total_log, local_state, "seq")
    carried = jnp.exp(cum_device).T[:, :, None] * jnp.einsum(
        "thn,hpn->thp", c_all.astype(jnp.float32), carry_in, precision=lax.Precision.HIGHEST
    )
    y_long = (
        y_blocks.reshape(tok_rows, head_count, HEADDIM)
        + carried
        + d_skip[None, :, None] * x_act.reshape(tok_rows, head_count, HEADDIM).astype(jnp.float32)
    )
    block_states = (jnp.exp(total_log)[:, None, None] * carry_in + local_state)[None]
    normed_long = gate_norm(y_long.reshape(tok_rows, inner_cols), z_long, norm_gain)
    is_valid = jnp.arange(SLEN)[None, :] < lengths[:, None]
    zero_x = jnp.zeros((req_count, rim_rows) + x_short.shape[2:], jnp.bfloat16)
    zero_bc = jnp.zeros((req_count, rim_rows) + bc_short.shape[2:], jnp.bfloat16)
    x_sact = jax.vmap(lambda item: conv_act(item, conv_x, conv_bias_x, SLEN))(
        jnp.concatenate([zero_x, x_short], 1)
    )
    bc_sact = jax.vmap(lambda item: conv_act(item, conv_bc, conv_bias_bc, SLEN))(
        jnp.concatenate([zero_bc, bc_short], 1)
    )
    dt_sfull = jax.nn.softplus(dt_short.astype(jnp.float32) + dt_bias[:, None, None]) * is_valid[
        None
    ].astype(jnp.float32)
    dt_sfull = dt_sfull.transpose(1, 0, 2)

    def per_request(x_req, bc_req, dt_req):
        return ssd_block(
            x_req.reshape(SLEN, head_count, HEADDIM),
            expand(bc_req[:, 0]),
            expand(bc_req[:, 1]),
            dt_req,
            decay_rate,
            start_state,
        )

    y_sblocks, short_states = jax.vmap(per_request)(x_sact, bc_sact, dt_sfull)
    y_short = y_sblocks + d_skip[None, None, :, None] * x_sact.reshape(
        req_count, SLEN, head_count, HEADDIM
    ).astype(jnp.float32)
    normed_short = gate_norm(
        y_short.reshape(req_count * SLEN, inner_cols),
        z_short.reshape(req_count * SLEN, inner_cols),
        norm_gain,
    )
    tail_pick = (
        jnp.arange(SLEN)[None, None, :]
        == (lengths[:, None] - rim_rows + jnp.arange(rim_rows)[None, :])[:, :, None]
    ).astype(jnp.float32)
    tails_x = jnp.einsum(
        "rks,rsc->rkc", tail_pick, x_short.astype(jnp.float32), precision=lax.Precision.HIGHEST
    ).astype(jnp.bfloat16)
    tails_bc = jnp.einsum(
        "rks,rsbc->rkbc", tail_pick, bc_short.astype(jnp.float32), precision=lax.Precision.HIGHEST
    ).astype(jnp.bfloat16)
    all_normed = jnp.concatenate([normed_long, normed_short], 0)
    tp_count = lax.axis_size("tp")
    tp_index = lax.axis_index("tp")
    width = out_weight.shape[1] // tp_count
    total = None
    for step in (2, 1, 3, 0):
        if step >= tp_count:
            continue
        target = (tp_index + step) % tp_count
        piece = lax.dynamic_slice_in_dim(out_weight, target * width, width, 1)
        term = jnp.dot(all_normed, piece, preferred_element_type=jnp.float32).astype(jnp.bfloat16)
        if step:
            term = lax.ppermute(
                term, "tp", [(i, (i + step) % tp_count) for i in range(tp_count)]
            )
        total = term.astype(jnp.float32) if total is None else total + term.astype(jnp.float32)
    hidden = total.astype(jnp.bfloat16)
    hidden_long = hidden[:tok_rows]
    hidden_short = hidden[tok_rows:].reshape(req_count, SLEN, -1) * is_valid[:, :, None].astype(
        jnp.bfloat16
    )
    last_pick = (jnp.arange(SLEN)[None, :] == lengths[:, None] - 1).astype(jnp.float32)
    short_last = jnp.einsum(
        "rs,rsc->rc",
        last_pick,
        normed_short.reshape(req_count, SLEN, inner_cols).astype(jnp.float32),
        precision=lax.Precision.HIGHEST,
    ).astype(jnp.bfloat16)
    short_rows = gather_all(tp_rows(short_last, out_weight), "seq", 0)
    short_norm = row_norm(short_rows, final_gain)
    short_top = jnp.max(
        lax.dot_general(
            short_norm, head_weight, (((1,), (1,)), ((), ())), preferred_element_type=jnp.float32
        ),
        axis=1,
    )
    y_last = (
        y_blocks[-1, BLOCK - 1]
        + jnp.exp(total_log)[:, None]
        * jnp.einsum(
            "hn,hpn->hp",
            c_all[tok_rows - 1].astype(jnp.float32),
            carry_in,
            precision=lax.Precision.HIGHEST,
        )
        + d_skip[:, None] * x_act[tok_rows - 1].reshape(head_count, HEADDIM).astype(jnp.float32)
    )
    normed_last = gate_norm(y_last.reshape(1, inner_cols), z_long[tok_rows - 1 :], norm_gain)
    long_row = from_last(tp_rows(normed_last, out_weight), "seq")
    long_norm = row_norm(long_row, final_gain)
    long_top = jnp.max(
        lax.dot_general(
            long_norm, head_weight, (((1,), (1,)), ((), ())), preferred_element_type=jnp.float32
        ),
        axis=1,
    )
    last_norm = jnp.concatenate([long_norm, short_norm], 0)
    top_logit = max_all(max_all(jnp.concatenate([long_top, short_top], 0), "tp"), "seq")
    return (
        hidden_long,
        hidden_short,
        block_states,
        short_states,
        tails_x,
        tails_bc,
        last_norm,
        top_logit,
    )


def solution(mesh):
    in_specs = (
        P("seq", "tp"),
        P("seq", None, "tp"),
        P("seq", "tp"),
        P("tp", "seq"),
        P("seq", None, "tp"),
        P("seq", None, None, "tp"),
        P("seq", None, "tp"),
        P("tp", "seq", None),
        P("seq"),
        P(None, "tp"),
        P(None, None, "tp"),
        P("tp"),
        P(None, "tp"),
        P("tp"),
        P("tp"),
        P("tp"),
        P("tp"),
        P("tp", None),
        P(),
        P(("seq", "tp"), None),
    )
    out_specs = (
        P("seq", "tp"),
        P("seq", None, "tp"),
        P("seq", "tp", None, None),
        P("seq", "tp", None, None),
        P("seq", None, "tp"),
        P("seq", None, None, "tp"),
        P(),
        P(),
    )
    return jax.shard_map(local, mesh=mesh, in_specs=in_specs, out_specs=out_specs, check_vma=False)
```

```python
import jax
import jax.numpy as jnp
from jax import lax
from jax.sharding import PartitionSpec as P

D = 4096
HEAD_SHARE = 64
HEADDIM = 64
GROUPS = 4
STATE = 128
KCONV = 4
BLOCK = 256
SLEN = 16


def passed_along(block, axis, distance):
    devices = range(lax.axis_size(axis))
    route = [(i - distance, i) for i in devices if i - distance in devices]
    return lax.ppermute(block, axis, route)


def swapped(block, axis, distance):
    devices = range(lax.axis_size(axis))
    return lax.ppermute(block, axis, [(i, i ^ distance) for i in devices])


def gather_all(block, axis, dim):
    count = lax.axis_size(axis)
    index = lax.axis_index(axis)
    distance = 1
    while distance < count:
        other = swapped(block, axis, distance)
        low = (index // distance) % 2 == 0
        block = jnp.where(
            low, jnp.concatenate([block, other], dim), jnp.concatenate([other, block], dim)
        )
        distance *= 2
    return block


def max_all(block, axis):
    distance = 1
    while distance < lax.axis_size(axis):
        block = jnp.maximum(block, swapped(block, axis, distance))
        distance *= 2
    return block


def tp_rows(rows, out_weight):
    part = jnp.dot(rows, out_weight, preferred_element_type=jnp.float32).astype(jnp.bfloat16)
    count = lax.axis_size("tp")
    index = lax.axis_index("tp")
    got = [part] + [
        lax.ppermute(part, "tp", [(i, (i + step) % count) for i in range(count)])
        for step in range(1, count)
    ]
    stacked = jnp.stack(got)
    total = jnp.zeros(part.shape, jnp.float32)
    for source in range(count):
        pick = lax.dynamic_index_in_dim(stacked, (index - source) % count, 0, keepdims=False)
        total = total + pick.astype(jnp.float32)
    return total.astype(jnp.bfloat16)


def row_norm(rows, final_gain):
    rows = rows.astype(jnp.float32)
    return (
        rows * lax.rsqrt(jnp.mean(rows * rows, axis=-1, keepdims=True) + 1e-05) * final_gain
    ).astype(jnp.bfloat16)


def carry_scan(total_log, local_state, axis):
    sent = local_state.astype(jnp.bfloat16)
    log_one, state_one = passed_along((total_log, sent), axis, 1)
    log_two, state_two = passed_along((total_log, sent), axis, 2)
    seg_log = log_one + log_two
    seg_state = jnp.exp(log_one)[:, None, None] * state_two.astype(jnp.float32) + state_one.astype(
        jnp.float32
    )
    distance = 2
    while distance < lax.axis_size(axis):
        got_log, got_state = passed_along(
            (seg_log, seg_state.astype(jnp.bfloat16)), axis, distance
        )
        seg_state = jnp.exp(seg_log)[:, None, None] * got_state.astype(jnp.float32) + seg_state
        seg_log = seg_log + got_log
        distance *= 2
    return seg_state


def conv_act(padded, weight, shift_bias, span_len):
    running_sum = shift_bias + 0.0 * padded[:span_len].astype(jnp.float32)
    for offset in range(weight.shape[0]):
        running_sum = running_sum + weight[offset] * padded[offset : offset + span_len].astype(
            jnp.float32
        )
    return jax.nn.silu(running_sum).astype(jnp.bfloat16)


def expand(portion):
    shaped = portion.reshape(portion.shape[:-1] + (portion.shape[-1] // STATE, STATE))
    return jnp.repeat(shaped, HEAD_SHARE // GROUPS, axis=-2)


def ssd_block(x_block, b_block, c_block, dt_block, decay_rate, state_in):
    step_log = dt_block * decay_rate[:, None]
    cumulative = jnp.cumsum(step_log, axis=1)
    span_len = x_block.shape[0]
    positions = jnp.arange(span_len)
    causal = (positions[:, None] >= positions[None, :])[None]
    log_gap = jnp.where(causal, cumulative[:, :, None] - cumulative[:, None, :], 0.0)
    decay_table = jnp.where(causal, jnp.exp(log_gap), 0.0)
    scores = jnp.einsum("thn,shn->hts", c_block, b_block, preferred_element_type=jnp.float32)
    weights = (scores * decay_table * dt_block[:, None, :]).astype(jnp.bfloat16)
    y_intra = jnp.einsum("hts,shp->thp", weights, x_block, preferred_element_type=jnp.float32)
    y_state = jnp.exp(cumulative).T[:, :, None] * jnp.einsum(
        "thn,hpn->thp", c_block.astype(jnp.float32), state_in, precision=lax.Precision.HIGHEST
    )
    to_end = jnp.exp(cumulative[:, -1:] - cumulative) * dt_block
    scaled = (x_block.astype(jnp.float32) * to_end.T[:, :, None]).astype(jnp.bfloat16)
    next_state = jnp.exp(cumulative[:, -1])[:, None, None] * state_in + jnp.einsum(
        "shp,shn->hpn", scaled, b_block, preferred_element_type=jnp.float32
    )
    return (y_intra + y_state, next_state)


def gate_norm(values, gating, scales):
    gated_rows = values * jax.nn.silu(gating.astype(jnp.float32))
    size_group = HEAD_SHARE // GROUPS * HEADDIM
    shaped = gated_rows.reshape(gated_rows.shape[0], -1, size_group)
    inv_rms = lax.rsqrt(jnp.mean(shaped * shaped, axis=-1, keepdims=True) + 1e-05)
    return ((shaped * inv_rms).reshape(gated_rows.shape) * scales).astype(jnp.bfloat16)


def local(
    x_long,
    bc_long,
    z_long,
    dt_long,
    x_short,
    bc_short,
    z_short,
    dt_short,
    lengths,
    conv_x,
    conv_bc,
    conv_bias_x,
    conv_bias_bc,
    dt_bias,
    a_log,
    d_skip,
    norm_gain,
    out_weight,
    final_gain,
    head_weight,
):
    tok_rows, inner_cols = x_long.shape
    head_count = dt_long.shape[0]
    req_count = lengths.shape[0]
    rim_rows = KCONV - 1
    decay_rate = -jnp.exp(a_log)
    rim_x, rim_bc = passed_along(
        (x_long[tok_rows - rim_rows :], bc_long[tok_rows - rim_rows :]), "seq", 1
    )
    x_act = conv_act(jnp.concatenate([rim_x, x_long], 0), conv_x, conv_bias_x, tok_rows)
    bc_act = conv_act(jnp.concatenate([rim_bc, bc_long], 0), conv_bc, conv_bias_bc, tok_rows)
    dt_full = jax.nn.softplus(dt_long.astype(jnp.float32) + dt_bias[:, None])
    block_count = tok_rows // BLOCK
    x_blocks = x_act.reshape(block_count, BLOCK, head_count, HEADDIM)
    b_blocks = expand(bc_act[:, 0]).reshape(block_count, BLOCK, head_count, STATE)
    c_all = expand(bc_act[:, 1])
    c_blocks = c_all.reshape(block_count, BLOCK, head_count, STATE)
    dt_blocks = dt_full.reshape(head_count, block_count, BLOCK).transpose(1, 0, 2)

    start_state = jnp.zeros((head_count, HEADDIM, STATE), jnp.float32)
    local_state = start_state
    y_parts = []
    for index in range(block_count):
        y_block, local_state = ssd_block(
            x_blocks[index], b_blocks[index], c_blocks[index], dt_blocks[index], decay_rate, local_state
        )
        y_parts.append(y_block)
    y_blocks = jnp.stack(y_parts)
    cum_device = jnp.cumsum(dt_full * decay_rate[:, None], axis=1)
    total_log = cum_device[:, -1]
    carry_in = carry_scan(total_log, local_state, "seq")
    carried = jnp.exp(cum_device).T[:, :, None] * jnp.einsum(
        "thn,hpn->thp", c_all.astype(jnp.float32), carry_in, precision=lax.Precision.HIGHEST
    )
    y_long = (
        y_blocks.reshape(tok_rows, head_count, HEADDIM)
        + carried
        + d_skip[None, :, None] * x_act.reshape(tok_rows, head_count, HEADDIM).astype(jnp.float32)
    )
    block_states = (jnp.exp(total_log)[:, None, None] * carry_in + local_state)[None]
    normed_long = gate_norm(y_long.reshape(tok_rows, inner_cols), z_long, norm_gain)
    is_valid = jnp.arange(SLEN)[None, :] < lengths[:, None]
    zero_x = jnp.zeros((req_count, rim_rows) + x_short.shape[2:], jnp.bfloat16)
    zero_bc = jnp.zeros((req_count, rim_rows) + bc_short.shape[2:], jnp.bfloat16)
    x_sact = jax.vmap(lambda item: conv_act(item, conv_x, conv_bias_x, SLEN))(
        jnp.concatenate([zero_x, x_short], 1)
    )
    bc_sact = jax.vmap(lambda item: conv_act(item, conv_bc, conv_bias_bc, SLEN))(
        jnp.concatenate([zero_bc, bc_short], 1)
    )
    dt_sfull = jax.nn.softplus(dt_short.astype(jnp.float32) + dt_bias[:, None, None]) * is_valid[
        None
    ].astype(jnp.float32)
    dt_sfull = dt_sfull.transpose(1, 0, 2)

    def per_request(x_req, bc_req, dt_req):
        return ssd_block(
            x_req.reshape(SLEN, head_count, HEADDIM),
            expand(bc_req[:, 0]),
            expand(bc_req[:, 1]),
            dt_req,
            decay_rate,
            start_state,
        )

    y_sblocks, short_states = jax.vmap(per_request)(x_sact, bc_sact, dt_sfull)
    y_short = y_sblocks + d_skip[None, None, :, None] * x_sact.reshape(
        req_count, SLEN, head_count, HEADDIM
    ).astype(jnp.float32)
    normed_short = gate_norm(
        y_short.reshape(req_count * SLEN, inner_cols),
        z_short.reshape(req_count * SLEN, inner_cols),
        norm_gain,
    )
    tail_pick = (
        jnp.arange(SLEN)[None, None, :]
        == (lengths[:, None] - rim_rows + jnp.arange(rim_rows)[None, :])[:, :, None]
    ).astype(jnp.float32)
    tails_x = jnp.einsum(
        "rks,rsc->rkc", tail_pick, x_short.astype(jnp.float32), precision=lax.Precision.HIGHEST
    ).astype(jnp.bfloat16)
    tails_bc = jnp.einsum(
        "rks,rsbc->rkbc", tail_pick, bc_short.astype(jnp.float32), precision=lax.Precision.HIGHEST
    ).astype(jnp.bfloat16)
    all_normed = jnp.concatenate([normed_long, normed_short], 0)
    tp_count = lax.axis_size("tp")
    tp_index = lax.axis_index("tp")
    width = out_weight.shape[1] // tp_count
    total = None
    for step in (2, 1, 3, 0):
        if step >= tp_count:
            continue
        target = (tp_index + step) % tp_count
        piece = lax.dynamic_slice_in_dim(out_weight, target * width, width, 1)
        term = jnp.dot(all_normed, piece, preferred_element_type=jnp.float32).astype(jnp.bfloat16)
        if step:
            term = lax.ppermute(
                term, "tp", [(i, (i + step) % tp_count) for i in range(tp_count)]
            )
        total = term.astype(jnp.float32) if total is None else total + term.astype(jnp.float32)
    hidden = total.astype(jnp.bfloat16)
    hidden_long = hidden[:tok_rows]
    hidden_short = hidden[tok_rows:].reshape(req_count, SLEN, -1) * is_valid[:, :, None].astype(
        jnp.bfloat16
    )
    last_pick = (jnp.arange(SLEN)[None, :] == lengths[:, None] - 1).astype(jnp.float32)
    short_last = jnp.einsum(
        "rs,rsc->rc",
        last_pick,
        normed_short.reshape(req_count, SLEN, inner_cols).astype(jnp.float32),
        precision=lax.Precision.HIGHEST,
    ).astype(jnp.bfloat16)
    y_last = (
        y_blocks[-1, BLOCK - 1]
        + jnp.exp(total_log)[:, None]
        * jnp.einsum(
            "hn,hpn->hp",
            c_all[tok_rows - 1].astype(jnp.float32),
            carry_in,
            precision=lax.Precision.HIGHEST,
        )
        + d_skip[:, None] * x_act[tok_rows - 1].reshape(head_count, HEADDIM).astype(jnp.float32)
    )
    normed_last = gate_norm(y_last.reshape(1, inner_cols), z_long[tok_rows - 1 :], norm_gain)
    rows = tp_rows(jnp.concatenate([short_last, normed_last], 0), out_weight)
    seq_count = lax.axis_size("seq")
    shaped = gather_all(rows, "seq", 0).reshape(seq_count, req_count + 1, D)
    long_row = shaped[seq_count - 1, req_count][None]
    short_all = shaped[:, :req_count].reshape(seq_count * req_count, D)
    last_norm = row_norm(jnp.concatenate([long_row, short_all], 0), final_gain)
    logits = lax.dot_general(
        last_norm, head_weight, (((1,), (1,)), ((), ())), preferred_element_type=jnp.float32
    )
    top_logit = max_all(max_all(jnp.max(logits, axis=1), "tp"), "seq")
    return (
        hidden_long,
        hidden_short,
        block_states,
        short_states,
        tails_x,
        tails_bc,
        last_norm,
        top_logit,
    )


def solution(mesh):
    in_specs = (
        P("seq", "tp"),
        P("seq", None, "tp"),
        P("seq", "tp"),
        P("tp", "seq"),
        P("seq", None, "tp"),
        P("seq", None, None, "tp"),
        P("seq", None, "tp"),
        P("tp", "seq", None),
        P("seq"),
        P(None, "tp"),
        P(None, None, "tp"),
        P("tp"),
        P(None, "tp"),
        P("tp"),
        P("tp"),
        P("tp"),
        P("tp"),
        P("tp", None),
        P(),
        P(("seq", "tp"), None),
    )
    out_specs = (
        P("seq", "tp"),
        P("seq", None, "tp"),
        P("seq", "tp", None, None),
        P("seq", "tp", None, None),
        P("seq", None, "tp"),
        P("seq", None, None, "tp"),
        P(),
        P(),
    )
    return jax.shard_map(local, mesh=mesh, in_specs=in_specs, out_specs=out_specs, check_vma=False)
```

```python
import jax
import jax.numpy as jnp
from jax import lax
from jax.sharding import PartitionSpec as P

D = 4096
HEAD_SHARE = 64
HEADDIM = 64
GROUPS = 4
STATE = 128
KCONV = 4
BLOCK = 256
SLEN = 16


def passed_along(block, axis, distance):
    devices = range(lax.axis_size(axis))
    route = [(i - distance, i) for i in devices if i - distance in devices]
    return lax.ppermute(block, axis, route)


def swapped(block, axis, distance):
    devices = range(lax.axis_size(axis))
    return lax.ppermute(block, axis, [(i, i ^ distance) for i in devices])


def gather_all(block, axis, dim):
    count = lax.axis_size(axis)
    index = lax.axis_index(axis)
    distance = 1
    while distance < count:
        other = swapped(block, axis, distance)
        low = (index // distance) % 2 == 0
        block = jnp.where(
            low, jnp.concatenate([block, other], dim), jnp.concatenate([other, block], dim)
        )
        distance *= 2
    return block


def max_all(block, axis):
    distance = 1
    while distance < lax.axis_size(axis):
        block = jnp.maximum(block, swapped(block, axis, distance))
        distance *= 2
    return block


def digit_route(count, distance, step, radix):
    route = []
    for i in range(count):
        digit = (i // distance) % radix
        route.append((i, i + ((digit + step) % radix - digit) * distance))
    return route


def gather_fast(block, axis, dim):
    count = lax.axis_size(axis)
    index = lax.axis_index(axis)
    distance = 1
    while distance < count:
        radix = min(4, count // distance)
        digit = (index // distance) % radix
        got = [block] + [
            lax.ppermute(block, axis, digit_route(count, distance, step, radix))
            for step in range(1, radix)
        ]
        stacked = jnp.stack(got)
        parts = [
            lax.dynamic_index_in_dim(stacked, (digit - part) % radix, 0, keepdims=False)
            for part in range(radix)
        ]
        block = jnp.concatenate(parts, dim)
        distance *= radix
    return block


def max_fast(block, axis):
    count = lax.axis_size(axis)
    distance = 1
    while distance < count:
        radix = min(4, count // distance)
        got = [
            lax.ppermute(block, axis, digit_route(count, distance, step, radix))
            for step in range(1, radix)
        ]
        for other in got:
            block = jnp.maximum(block, other)
        distance *= radix
    return block


def carry_scan(total_log, local_state, axis):
    sent = local_state.astype(jnp.bfloat16)
    log_one, state_one = passed_along((total_log, sent), axis, 1)
    log_two, state_two = passed_along((total_log, sent), axis, 2)
    seg_log = log_one + log_two
    seg_state = jnp.exp(log_one)[:, None, None] * state_two.astype(jnp.float32) + state_one.astype(
        jnp.float32
    )
    distance = 2
    while distance < lax.axis_size(axis):
        got_log, got_state = passed_along(
            (seg_log, seg_state.astype(jnp.bfloat16)), axis, distance
        )
        seg_state = jnp.exp(seg_log)[:, None, None] * got_state.astype(jnp.float32) + seg_state
        seg_log = seg_log + got_log
        distance *= 2
    return seg_state


def conv_act(padded, weight, shift_bias, span_len):
    running_sum = shift_bias + 0.0 * padded[:span_len].astype(jnp.float32)
    for offset in range(weight.shape[0]):
        running_sum = running_sum + weight[offset] * padded[offset : offset + span_len].astype(
            jnp.float32
        )
    return jax.nn.silu(running_sum).astype(jnp.bfloat16)


def expand(portion):
    shaped = portion.reshape(portion.shape[:-1] + (portion.shape[-1] // STATE, STATE))
    return jnp.repeat(shaped, HEAD_SHARE // GROUPS, axis=-2)


def ssd_block(x_block, b_block, c_block, dt_block, decay_rate, state_in):
    step_log = dt_block * decay_rate[:, None]
    cumulative = jnp.cumsum(step_log, axis=1)
    span_len = x_block.shape[0]
    positions = jnp.arange(span_len)
    causal = (positions[:, None] >= positions[None, :])[None]
    log_gap = jnp.where(causal, cumulative[:, :, None] - cumulative[:, None, :], 0.0)
    decay_table = jnp.where(causal, jnp.exp(log_gap), 0.0)
    scores = jnp.einsum("thn,shn->hts", c_block, b_block, preferred_element_type=jnp.float32)
    weights = (scores * decay_table * dt_block[:, None, :]).astype(jnp.bfloat16)
    y_intra = jnp.einsum("hts,shp->thp", weights, x_block, preferred_element_type=jnp.float32)
    y_state = jnp.exp(cumulative).T[:, :, None] * jnp.einsum(
        "thn,hpn->thp", c_block.astype(jnp.float32), state_in, precision=lax.Precision.HIGHEST
    )
    to_end = jnp.exp(cumulative[:, -1:] - cumulative) * dt_block
    scaled = (x_block.astype(jnp.float32) * to_end.T[:, :, None]).astype(jnp.bfloat16)
    next_state = jnp.exp(cumulative[:, -1])[:, None, None] * state_in + jnp.einsum(
        "shp,shn->hpn", scaled, b_block, preferred_element_type=jnp.float32
    )
    return (y_intra + y_state, next_state)


def gate_norm(values, gating, scales):
    gated_rows = values * jax.nn.silu(gating.astype(jnp.float32))
    size_group = HEAD_SHARE // GROUPS * HEADDIM
    shaped = gated_rows.reshape(gated_rows.shape[0], -1, size_group)
    inv_rms = lax.rsqrt(jnp.mean(shaped * shaped, axis=-1, keepdims=True) + 1e-05)
    return ((shaped * inv_rms).reshape(gated_rows.shape) * scales).astype(jnp.bfloat16)


def local(
    x_long,
    bc_long,
    z_long,
    dt_long,
    x_short,
    bc_short,
    z_short,
    dt_short,
    lengths,
    conv_x,
    conv_bc,
    conv_bias_x,
    conv_bias_bc,
    dt_bias,
    a_log,
    d_skip,
    norm_gain,
    out_weight,
    final_gain,
    head_weight,
):
    tok_rows, inner_cols = x_long.shape
    head_count = dt_long.shape[0]
    req_count = lengths.shape[0]
    rim_rows = KCONV - 1
    decay_rate = -jnp.exp(a_log)
    rim_x, rim_bc = passed_along(
        (x_long[tok_rows - rim_rows :], bc_long[tok_rows - rim_rows :]), "seq", 1
    )
    x_act = conv_act(jnp.concatenate([rim_x, x_long], 0), conv_x, conv_bias_x, tok_rows)
    bc_act = conv_act(jnp.concatenate([rim_bc, bc_long], 0), conv_bc, conv_bias_bc, tok_rows)
    dt_full = jax.nn.softplus(dt_long.astype(jnp.float32) + dt_bias[:, None])
    block_count = tok_rows // BLOCK
    x_blocks = x_act.reshape(block_count, BLOCK, head_count, HEADDIM)
    b_blocks = expand(bc_act[:, 0]).reshape(block_count, BLOCK, head_count, STATE)
    c_all = expand(bc_act[:, 1])
    c_blocks = c_all.reshape(block_count, BLOCK, head_count, STATE)
    dt_blocks = dt_full.reshape(head_count, block_count, BLOCK).transpose(1, 0, 2)

    start_state = jnp.zeros((head_count, HEADDIM, STATE), jnp.float32)
    local_state = start_state
    y_parts = []
    for index in range(block_count):
        y_block, local_state = ssd_block(
            x_blocks[index], b_blocks[index], c_blocks[index], dt_blocks[index], decay_rate, local_state
        )
        y_parts.append(y_block)
    y_blocks = jnp.stack(y_parts)
    cum_device = jnp.cumsum(dt_full * decay_rate[:, None], axis=1)
    total_log = cum_device[:, -1]
    carry_in = carry_scan(total_log, local_state, "seq")
    carried = jnp.exp(cum_device).T[:, :, None] * jnp.einsum(
        "thn,hpn->thp", c_all.astype(jnp.float32), carry_in, precision=lax.Precision.HIGHEST
    )
    y_long = (
        y_blocks.reshape(tok_rows, head_count, HEADDIM)
        + carried
        + d_skip[None, :, None] * x_act.reshape(tok_rows, head_count, HEADDIM).astype(jnp.float32)
    )
    block_states = (jnp.exp(total_log)[:, None, None] * carry_in + local_state)[None]
    normed_long = gate_norm(y_long.reshape(tok_rows, inner_cols), z_long, norm_gain)
    is_valid = jnp.arange(SLEN)[None, :] < lengths[:, None]
    zero_x = jnp.zeros((req_count, rim_rows) + x_short.shape[2:], jnp.bfloat16)
    zero_bc = jnp.zeros((req_count, rim_rows) + bc_short.shape[2:], jnp.bfloat16)
    x_sact = jax.vmap(lambda item: conv_act(item, conv_x, conv_bias_x, SLEN))(
        jnp.concatenate([zero_x, x_short], 1)
    )
    bc_sact = jax.vmap(lambda item: conv_act(item, conv_bc, conv_bias_bc, SLEN))(
        jnp.concatenate([zero_bc, bc_short], 1)
    )
    dt_sfull = jax.nn.softplus(dt_short.astype(jnp.float32) + dt_bias[:, None, None]) * is_valid[
        None
    ].astype(jnp.float32)
    dt_sfull = dt_sfull.transpose(1, 0, 2)

    def per_request(x_req, bc_req, dt_req):
        return ssd_block(
            x_req.reshape(SLEN, head_count, HEADDIM),
            expand(bc_req[:, 0]),
            expand(bc_req[:, 1]),
            dt_req,
            decay_rate,
            start_state,
        )

    y_sblocks, short_states = jax.vmap(per_request)(x_sact, bc_sact, dt_sfull)
    y_short = y_sblocks + d_skip[None, None, :, None] * x_sact.reshape(
        req_count, SLEN, head_count, HEADDIM
    ).astype(jnp.float32)
    normed_short = gate_norm(
        y_short.reshape(req_count * SLEN, inner_cols),
        z_short.reshape(req_count * SLEN, inner_cols),
        norm_gain,
    )
    tail_pick = (
        jnp.arange(SLEN)[None, None, :]
        == (lengths[:, None] - rim_rows + jnp.arange(rim_rows)[None, :])[:, :, None]
    ).astype(jnp.float32)
    tails_x = jnp.einsum(
        "rks,rsc->rkc", tail_pick, x_short.astype(jnp.float32), precision=lax.Precision.HIGHEST
    ).astype(jnp.bfloat16)
    tails_bc = jnp.einsum(
        "rks,rsbc->rkbc", tail_pick, bc_short.astype(jnp.float32), precision=lax.Precision.HIGHEST
    ).astype(jnp.bfloat16)
    all_normed = jnp.concatenate([normed_long, normed_short], 0)
    tp_count = lax.axis_size("tp")
    tp_index = lax.axis_index("tp")
    width = out_weight.shape[1] // tp_count
    total = None
    for step in (2, 1, 3, 0):
        if step >= tp_count:
            continue
        target = (tp_index + step) % tp_count
        piece = lax.dynamic_slice_in_dim(out_weight, target * width, width, 1)
        term = jnp.dot(all_normed, piece, preferred_element_type=jnp.float32).astype(jnp.bfloat16)
        if step:
            term = lax.ppermute(
                term, "tp", [(i, (i + step) % tp_count) for i in range(tp_count)]
            )
        total = term.astype(jnp.float32) if total is None else total + term.astype(jnp.float32)
    hidden = total.astype(jnp.bfloat16)
    hidden_long = hidden[:tok_rows]
    hidden_short = hidden[tok_rows:].reshape(req_count, SLEN, -1) * is_valid[:, :, None].astype(
        jnp.bfloat16
    )
    last_pick = (jnp.arange(SLEN)[None, :] == lengths[:, None] - 1).astype(jnp.float32)
    short_rows = jnp.einsum(
        "rs,rsd->rd", last_pick, hidden_short.astype(jnp.float32), precision=lax.Precision.HIGHEST
    ).astype(jnp.bfloat16)
    packed = jnp.concatenate([short_rows, hidden_long[tok_rows - 1 :]], 0)
    seq_rows = gather_fast(packed, "seq", 0)
    full_rows = gather_fast(seq_rows, "tp", 1)
    seq_count = lax.axis_size("seq")
    shaped = full_rows.reshape(seq_count, req_count + 1, D)
    long_row = shaped[seq_count - 1, req_count][None]
    short_all = shaped[:, :req_count].reshape(seq_count * req_count, D)
    row_block = jnp.concatenate([long_row, short_all], 0).astype(jnp.float32)
    last_norm = (
        row_block
        * lax.rsqrt(jnp.mean(row_block * row_block, axis=-1, keepdims=True) + 1e-05)
        * final_gain
    ).astype(jnp.bfloat16)
    logits = lax.dot_general(
        last_norm, head_weight, (((1,), (1,)), ((), ())), preferred_element_type=jnp.float32
    )
    top_logit = max_fast(max_fast(jnp.max(logits, axis=1), "tp"), "seq")
    return (
        hidden_long,
        hidden_short,
        block_states,
        short_states,
        tails_x,
        tails_bc,
        last_norm,
        top_logit,
    )


def solution(mesh):
    in_specs = (
        P("seq", "tp"),
        P("seq", None, "tp"),
        P("seq", "tp"),
        P("tp", "seq"),
        P("seq", None, "tp"),
        P("seq", None, None, "tp"),
        P("seq", None, "tp"),
        P("tp", "seq", None),
        P("seq"),
        P(None, "tp"),
        P(None, None, "tp"),
        P("tp"),
        P(None, "tp"),
        P("tp"),
        P("tp"),
        P("tp"),
        P("tp"),
        P("tp", None),
        P(),
        P(("seq", "tp"), None),
    )
    out_specs = (
        P("seq", "tp"),
        P("seq", None, "tp"),
        P("seq", "tp", None, None),
        P("seq", "tp", None, None),
        P("seq", None, "tp"),
        P("seq", None, None, "tp"),
        P(),
        P(),
    )
    return jax.shard_map(local, mesh=mesh, in_specs=in_specs, out_specs=out_specs, check_vma=False)
```

```python
import jax
import jax.numpy as jnp
from jax import lax
from jax.sharding import PartitionSpec as P

D = 4096
HEAD_SHARE = 64
HEADDIM = 64
GROUPS = 4
STATE = 128
KCONV = 4
BLOCK = 256
SLEN = 16


def passed_along(block, axis, distance):
    devices = range(lax.axis_size(axis))
    route = [(i - distance, i) for i in devices if i - distance in devices]
    return lax.ppermute(block, axis, route)


def swapped(block, axis, distance):
    devices = range(lax.axis_size(axis))
    return lax.ppermute(block, axis, [(i, i ^ distance) for i in devices])


def gather_all(block, axis, dim):
    count = lax.axis_size(axis)
    index = lax.axis_index(axis)
    distance = 1
    while distance < count:
        other = swapped(block, axis, distance)
        low = (index // distance) % 2 == 0
        block = jnp.where(
            low, jnp.concatenate([block, other], dim), jnp.concatenate([other, block], dim)
        )
        distance *= 2
    return block


def max_all(block, axis):
    distance = 1
    while distance < lax.axis_size(axis):
        block = jnp.maximum(block, swapped(block, axis, distance))
        distance *= 2
    return block


def digit_route(count, distance, step, radix):
    route = []
    for i in range(count):
        digit = (i // distance) % radix
        route.append((i, i + ((digit + step) % radix - digit) * distance))
    return route


def gather_fast(block, axis, dim):
    count = lax.axis_size(axis)
    index = lax.axis_index(axis)
    distance = 1
    while distance < count:
        radix = min(4, count // distance)
        digit = (index // distance) % radix
        got = [block] + [
            lax.ppermute(block, axis, digit_route(count, distance, step, radix))
            for step in range(1, radix)
        ]
        stacked = jnp.stack(got)
        parts = [
            lax.dynamic_index_in_dim(stacked, (digit - part) % radix, 0, keepdims=False)
            for part in range(radix)
        ]
        block = jnp.concatenate(parts, dim)
        distance *= radix
    return block


def max_fast(block, axis):
    count = lax.axis_size(axis)
    distance = 1
    while distance < count:
        radix = min(4, count // distance)
        got = [
            lax.ppermute(block, axis, digit_route(count, distance, step, radix))
            for step in range(1, radix)
        ]
        for other in got:
            block = jnp.maximum(block, other)
        distance *= radix
    return block


def pack(state, log):
    heads = log.shape[0]
    high = log.astype(jnp.bfloat16)
    rest = log - high.astype(jnp.float32)
    mid = rest.astype(jnp.bfloat16)
    low = (rest - mid.astype(jnp.float32)).astype(jnp.bfloat16)
    lanes = state.shape[-1]
    row = jnp.concatenate([high, mid, low, jnp.zeros((lanes - 3 * heads,), jnp.bfloat16)])
    flat = state.astype(jnp.bfloat16).reshape(-1, lanes)
    return jnp.concatenate([flat, row[None]], 0)


def unpack(message, heads):
    lanes = message.shape[-1]
    state = message[:-1].reshape(heads, -1, lanes).astype(jnp.float32)
    row = message[-1].astype(jnp.float32)
    log = (row[:heads] + row[heads : 2 * heads]) + row[2 * heads : 3 * heads]
    return log, state


def carry_scan(total_log, local_state, axis):
    heads = total_log.shape[0]
    sent = pack(local_state, total_log)
    log_one, state_one = unpack(passed_along(sent, axis, 1), heads)
    log_two, state_two = unpack(passed_along(sent, axis, 2), heads)
    seg_log = log_one + log_two
    seg_state = jnp.exp(log_one)[:, None, None] * state_two + state_one
    distance = 2
    while distance < lax.axis_size(axis):
        got_log, got_state = unpack(passed_along(pack(seg_state, seg_log), axis, distance), heads)
        seg_state = jnp.exp(seg_log)[:, None, None] * got_state + seg_state
        seg_log = seg_log + got_log
        distance *= 2
    return seg_state


def conv_act(padded, weight, shift_bias, span_len):
    running_sum = shift_bias + 0.0 * padded[:span_len].astype(jnp.float32)
    for offset in range(weight.shape[0]):
        running_sum = running_sum + weight[offset] * padded[offset : offset + span_len].astype(
            jnp.float32
        )
    return jax.nn.silu(running_sum).astype(jnp.bfloat16)


def expand(portion):
    shaped = portion.reshape(portion.shape[:-1] + (portion.shape[-1] // STATE, STATE))
    return jnp.repeat(shaped, HEAD_SHARE // GROUPS, axis=-2)


def ssd_block(x_block, b_block, c_block, dt_block, decay_rate, state_in):
    step_log = dt_block * decay_rate[:, None]
    cumulative = jnp.cumsum(step_log, axis=1)
    span_len = x_block.shape[0]
    positions = jnp.arange(span_len)
    causal = (positions[:, None] >= positions[None, :])[None]
    log_gap = jnp.where(causal, cumulative[:, :, None] - cumulative[:, None, :], 0.0)
    decay_table = jnp.where(causal, jnp.exp(log_gap), 0.0)
    scores = jnp.einsum("thn,shn->hts", c_block, b_block, preferred_element_type=jnp.float32)
    weights = (scores * decay_table * dt_block[:, None, :]).astype(jnp.bfloat16)
    y_intra = jnp.einsum("hts,shp->thp", weights, x_block, preferred_element_type=jnp.float32)
    y_state = jnp.exp(cumulative).T[:, :, None] * jnp.einsum(
        "thn,hpn->thp", c_block.astype(jnp.float32), state_in, precision=lax.Precision.HIGHEST
    )
    to_end = jnp.exp(cumulative[:, -1:] - cumulative) * dt_block
    scaled = (x_block.astype(jnp.float32) * to_end.T[:, :, None]).astype(jnp.bfloat16)
    next_state = jnp.exp(cumulative[:, -1])[:, None, None] * state_in + jnp.einsum(
        "shp,shn->hpn", scaled, b_block, preferred_element_type=jnp.float32
    )
    return (y_intra + y_state, next_state)


def gate_norm(values, gating, scales):
    gated_rows = values * jax.nn.silu(gating.astype(jnp.float32))
    size_group = HEAD_SHARE // GROUPS * HEADDIM
    shaped = gated_rows.reshape(gated_rows.shape[0], -1, size_group)
    inv_rms = lax.rsqrt(jnp.mean(shaped * shaped, axis=-1, keepdims=True) + 1e-05)
    return ((shaped * inv_rms).reshape(gated_rows.shape) * scales).astype(jnp.bfloat16)


def local(
    x_long,
    bc_long,
    z_long,
    dt_long,
    x_short,
    bc_short,
    z_short,
    dt_short,
    lengths,
    conv_x,
    conv_bc,
    conv_bias_x,
    conv_bias_bc,
    dt_bias,
    a_log,
    d_skip,
    norm_gain,
    out_weight,
    final_gain,
    head_weight,
):
    tok_rows, inner_cols = x_long.shape
    head_count = dt_long.shape[0]
    req_count = lengths.shape[0]
    rim_rows = KCONV - 1
    decay_rate = -jnp.exp(a_log)
    rim_x, rim_bc = passed_along(
        (x_long[tok_rows - rim_rows :], bc_long[tok_rows - rim_rows :]), "seq", 1
    )
    x_act = conv_act(jnp.concatenate([rim_x, x_long], 0), conv_x, conv_bias_x, tok_rows)
    bc_act = conv_act(jnp.concatenate([rim_bc, bc_long], 0), conv_bc, conv_bias_bc, tok_rows)
    dt_full = jax.nn.softplus(dt_long.astype(jnp.float32) + dt_bias[:, None])
    block_count = tok_rows // BLOCK
    x_blocks = x_act.reshape(block_count, BLOCK, head_count, HEADDIM)
    b_blocks = expand(bc_act[:, 0]).reshape(block_count, BLOCK, head_count, STATE)
    c_all = expand(bc_act[:, 1])
    c_blocks = c_all.reshape(block_count, BLOCK, head_count, STATE)
    dt_blocks = dt_full.reshape(head_count, block_count, BLOCK).transpose(1, 0, 2)

    start_state = jnp.zeros((head_count, HEADDIM, STATE), jnp.float32)
    local_state = start_state
    y_parts = []
    for index in range(block_count):
        y_block, local_state = ssd_block(
            x_blocks[index], b_blocks[index], c_blocks[index], dt_blocks[index], decay_rate, local_state
        )
        y_parts.append(y_block)
    y_blocks = jnp.stack(y_parts)
    cum_device = jnp.cumsum(dt_full * decay_rate[:, None], axis=1)
    total_log = cum_device[:, -1]
    carry_in = carry_scan(total_log, local_state, "seq")
    carried = jnp.exp(cum_device).T[:, :, None] * jnp.einsum(
        "thn,hpn->thp", c_all.astype(jnp.float32), carry_in, precision=lax.Precision.HIGHEST
    )
    y_long = (
        y_blocks.reshape(tok_rows, head_count, HEADDIM)
        + carried
        + d_skip[None, :, None] * x_act.reshape(tok_rows, head_count, HEADDIM).astype(jnp.float32)
    )
    block_states = (jnp.exp(total_log)[:, None, None] * carry_in + local_state)[None]
    normed_long = gate_norm(y_long.reshape(tok_rows, inner_cols), z_long, norm_gain)
    is_valid = jnp.arange(SLEN)[None, :] < lengths[:, None]
    zero_x = jnp.zeros((req_count, rim_rows) + x_short.shape[2:], jnp.bfloat16)
    zero_bc = jnp.zeros((req_count, rim_rows) + bc_short.shape[2:], jnp.bfloat16)
    x_sact = jax.vmap(lambda item: conv_act(item, conv_x, conv_bias_x, SLEN))(
        jnp.concatenate([zero_x, x_short], 1)
    )
    bc_sact = jax.vmap(lambda item: conv_act(item, conv_bc, conv_bias_bc, SLEN))(
        jnp.concatenate([zero_bc, bc_short], 1)
    )
    dt_sfull = jax.nn.softplus(dt_short.astype(jnp.float32) + dt_bias[:, None, None]) * is_valid[
        None
    ].astype(jnp.float32)
    dt_sfull = dt_sfull.transpose(1, 0, 2)

    def per_request(x_req, bc_req, dt_req):
        return ssd_block(
            x_req.reshape(SLEN, head_count, HEADDIM),
            expand(bc_req[:, 0]),
            expand(bc_req[:, 1]),
            dt_req,
            decay_rate,
            start_state,
        )

    y_sblocks, short_states = jax.vmap(per_request)(x_sact, bc_sact, dt_sfull)
    y_short = y_sblocks + d_skip[None, None, :, None] * x_sact.reshape(
        req_count, SLEN, head_count, HEADDIM
    ).astype(jnp.float32)
    normed_short = gate_norm(
        y_short.reshape(req_count * SLEN, inner_cols),
        z_short.reshape(req_count * SLEN, inner_cols),
        norm_gain,
    )
    tail_pick = (
        jnp.arange(SLEN)[None, None, :]
        == (lengths[:, None] - rim_rows + jnp.arange(rim_rows)[None, :])[:, :, None]
    ).astype(jnp.float32)
    tails_x = jnp.einsum(
        "rks,rsc->rkc", tail_pick, x_short.astype(jnp.float32), precision=lax.Precision.HIGHEST
    ).astype(jnp.bfloat16)
    tails_bc = jnp.einsum(
        "rks,rsbc->rkbc", tail_pick, bc_short.astype(jnp.float32), precision=lax.Precision.HIGHEST
    ).astype(jnp.bfloat16)
    all_normed = jnp.concatenate([normed_long, normed_short], 0)
    tp_count = lax.axis_size("tp")
    tp_index = lax.axis_index("tp")
    width = out_weight.shape[1] // tp_count
    total = None
    for step in (2, 1, 3, 0):
        if step >= tp_count:
            continue
        target = (tp_index + step) % tp_count
        piece = lax.dynamic_slice_in_dim(out_weight, target * width, width, 1)
        term = jnp.dot(all_normed, piece, preferred_element_type=jnp.float32).astype(jnp.bfloat16)
        if step:
            term = lax.ppermute(
                term, "tp", [(i, (i + step) % tp_count) for i in range(tp_count)]
            )
        total = term.astype(jnp.float32) if total is None else total + term.astype(jnp.float32)
    hidden = total.astype(jnp.bfloat16)
    hidden_long = hidden[:tok_rows]
    hidden_short = hidden[tok_rows:].reshape(req_count, SLEN, -1) * is_valid[:, :, None].astype(
        jnp.bfloat16
    )
    last_pick = (jnp.arange(SLEN)[None, :] == lengths[:, None] - 1).astype(jnp.float32)
    short_rows = jnp.einsum(
        "rs,rsd->rd", last_pick, hidden_short.astype(jnp.float32), precision=lax.Precision.HIGHEST
    ).astype(jnp.bfloat16)
    packed = jnp.concatenate([short_rows, hidden_long[tok_rows - 1 :]], 0)
    seq_rows = gather_fast(packed, "seq", 0)
    full_rows = gather_fast(seq_rows, "tp", 1)
    seq_count = lax.axis_size("seq")
    shaped = full_rows.reshape(seq_count, req_count + 1, D)
    long_row = shaped[seq_count - 1, req_count][None]
    short_all = shaped[:, :req_count].reshape(seq_count * req_count, D)
    row_block = jnp.concatenate([long_row, short_all], 0).astype(jnp.float32)
    last_norm = (
        row_block
        * lax.rsqrt(jnp.mean(row_block * row_block, axis=-1, keepdims=True) + 1e-05)
        * final_gain
    ).astype(jnp.bfloat16)
    logits = lax.dot_general(
        last_norm, head_weight, (((1,), (1,)), ((), ())), preferred_element_type=jnp.float32
    )
    top_logit = max_fast(max_fast(jnp.max(logits, axis=1), "tp"), "seq")
    return (
        hidden_long,
        hidden_short,
        block_states,
        short_states,
        tails_x,
        tails_bc,
        last_norm,
        top_logit,
    )


def solution(mesh):
    in_specs = (
        P("seq", "tp"),
        P("seq", None, "tp"),
        P("seq", "tp"),
        P("tp", "seq"),
        P("seq", None, "tp"),
        P("seq", None, None, "tp"),
        P("seq", None, "tp"),
        P("tp", "seq", None),
        P("seq"),
        P(None, "tp"),
        P(None, None, "tp"),
        P("tp"),
        P(None, "tp"),
        P("tp"),
        P("tp"),
        P("tp"),
        P("tp"),
        P("tp", None),
        P(),
        P(("seq", "tp"), None),
    )
    out_specs = (
        P("seq", "tp"),
        P("seq", None, "tp"),
        P("seq", "tp", None, None),
        P("seq", "tp", None, None),
        P("seq", None, "tp"),
        P("seq", None, None, "tp"),
        P(),
        P(),
    )
    return jax.shard_map(local, mesh=mesh, in_specs=in_specs, out_specs=out_specs, check_vma=False)
```

```python
import jax
import jax.numpy as jnp
from jax import lax
from jax.sharding import PartitionSpec as P

D = 4096
HEAD_SHARE = 64
HEADDIM = 64
GROUPS = 4
STATE = 128
KCONV = 4
BLOCK = 256
SLEN = 16


def passed_along(block, axis, distance):
    devices = range(lax.axis_size(axis))
    route = [(i - distance, i) for i in devices if i - distance in devices]
    return lax.ppermute(block, axis, route)


def swapped(block, axis, distance):
    devices = range(lax.axis_size(axis))
    return lax.ppermute(block, axis, [(i, i ^ distance) for i in devices])


def gather_all(block, axis, dim):
    count = lax.axis_size(axis)
    index = lax.axis_index(axis)
    distance = 1
    while distance < count:
        other = swapped(block, axis, distance)
        low = (index // distance) % 2 == 0
        block = jnp.where(
            low, jnp.concatenate([block, other], dim), jnp.concatenate([other, block], dim)
        )
        distance *= 2
    return block


def max_all(block, axis):
    distance = 1
    while distance < lax.axis_size(axis):
        block = jnp.maximum(block, swapped(block, axis, distance))
        distance *= 2
    return block


def digit_route(count, distance, step, radix):
    route = []
    for i in range(count):
        digit = (i // distance) % radix
        route.append((i, i + ((digit + step) % radix - digit) * distance))
    return route


def gather_fast(block, axis, dim):
    count = lax.axis_size(axis)
    index = lax.axis_index(axis)
    distance = 1
    while distance < count:
        radix = min(4, count // distance)
        digit = (index // distance) % radix
        got = [block] + [
            lax.ppermute(block, axis, digit_route(count, distance, step, radix))
            for step in range(1, radix)
        ]
        stacked = jnp.stack(got)
        parts = [
            lax.dynamic_index_in_dim(stacked, (digit - part) % radix, 0, keepdims=False)
            for part in range(radix)
        ]
        block = jnp.concatenate(parts, dim)
        distance *= radix
    return block


def max_fast(block, axis):
    count = lax.axis_size(axis)
    distance = 1
    while distance < count:
        radix = min(4, count // distance)
        got = [
            lax.ppermute(block, axis, digit_route(count, distance, step, radix))
            for step in range(1, radix)
        ]
        for other in got:
            block = jnp.maximum(block, other)
        distance *= radix
    return block


def tp_rows(rows, out_weight):
    part = jnp.dot(rows, out_weight, preferred_element_type=jnp.float32).astype(jnp.bfloat16)
    count = lax.axis_size("tp")
    index = lax.axis_index("tp")
    got = [part] + [
        lax.ppermute(part, "tp", [(i, (i + step) % count) for i in range(count)])
        for step in range(1, count)
    ]
    stacked = jnp.stack(got)
    total = jnp.zeros(part.shape, jnp.float32)
    for source in range(count):
        pick = lax.dynamic_index_in_dim(stacked, (index - source) % count, 0, keepdims=False)
        total = total + pick.astype(jnp.float32)
    return total.astype(jnp.bfloat16)


def row_norm(rows, final_gain):
    rows = rows.astype(jnp.float32)
    return (
        rows * lax.rsqrt(jnp.mean(rows * rows, axis=-1, keepdims=True) + 1e-05) * final_gain
    ).astype(jnp.bfloat16)


def pack(state, log):
    heads = log.shape[0]
    high = log.astype(jnp.bfloat16)
    rest = log - high.astype(jnp.float32)
    mid = rest.astype(jnp.bfloat16)
    low = (rest - mid.astype(jnp.float32)).astype(jnp.bfloat16)
    lanes = state.shape[-1]
    row = jnp.concatenate([high, mid, low, jnp.zeros((lanes - 3 * heads,), jnp.bfloat16)])
    flat = state.astype(jnp.bfloat16).reshape(-1, lanes)
    return jnp.concatenate([flat, row[None]], 0)


def unpack(message, heads):
    lanes = message.shape[-1]
    state = message[:-1].reshape(heads, -1, lanes).astype(jnp.float32)
    row = message[-1].astype(jnp.float32)
    log = (row[:heads] + row[heads : 2 * heads]) + row[2 * heads : 3 * heads]
    return log, state


def carry_scan(total_log, local_state, axis):
    heads = total_log.shape[0]
    sent = pack(local_state, total_log)
    log_one, state_one = unpack(passed_along(sent, axis, 1), heads)
    log_two, state_two = unpack(passed_along(sent, axis, 2), heads)
    seg_log = log_one + log_two
    seg_state = jnp.exp(log_one)[:, None, None] * state_two + state_one
    distance = 2
    while distance < lax.axis_size(axis):
        got_log, got_state = unpack(passed_along(pack(seg_state, seg_log), axis, distance), heads)
        seg_state = jnp.exp(seg_log)[:, None, None] * got_state + seg_state
        seg_log = seg_log + got_log
        distance *= 2
    return seg_state


def conv_act(padded, weight, shift_bias, span_len):
    running_sum = shift_bias + 0.0 * padded[:span_len].astype(jnp.float32)
    for offset in range(weight.shape[0]):
        running_sum = running_sum + weight[offset] * padded[offset : offset + span_len].astype(
            jnp.float32
        )
    return jax.nn.silu(running_sum).astype(jnp.bfloat16)


def expand(portion):
    shaped = portion.reshape(portion.shape[:-1] + (portion.shape[-1] // STATE, STATE))
    return jnp.repeat(shaped, HEAD_SHARE // GROUPS, axis=-2)


def ssd_block(x_block, b_block, c_block, dt_block, decay_rate, state_in):
    step_log = dt_block * decay_rate[:, None]
    cumulative = jnp.cumsum(step_log, axis=1)
    span_len = x_block.shape[0]
    positions = jnp.arange(span_len)
    causal = (positions[:, None] >= positions[None, :])[None]
    log_gap = jnp.where(causal, cumulative[:, :, None] - cumulative[:, None, :], 0.0)
    decay_table = jnp.where(causal, jnp.exp(log_gap), 0.0)
    scores = jnp.einsum("thn,shn->hts", c_block, b_block, preferred_element_type=jnp.float32)
    weights = (scores * decay_table * dt_block[:, None, :]).astype(jnp.bfloat16)
    y_intra = jnp.einsum("hts,shp->thp", weights, x_block, preferred_element_type=jnp.float32)
    y_state = jnp.exp(cumulative).T[:, :, None] * jnp.einsum(
        "thn,hpn->thp", c_block.astype(jnp.float32), state_in, precision=lax.Precision.HIGHEST
    )
    to_end = jnp.exp(cumulative[:, -1:] - cumulative) * dt_block
    scaled = (x_block.astype(jnp.float32) * to_end.T[:, :, None]).astype(jnp.bfloat16)
    next_state = jnp.exp(cumulative[:, -1])[:, None, None] * state_in + jnp.einsum(
        "shp,shn->hpn", scaled, b_block, preferred_element_type=jnp.float32
    )
    return (y_intra + y_state, next_state)


def gate_norm(values, gating, scales):
    gated_rows = values * jax.nn.silu(gating.astype(jnp.float32))
    size_group = HEAD_SHARE // GROUPS * HEADDIM
    shaped = gated_rows.reshape(gated_rows.shape[0], -1, size_group)
    inv_rms = lax.rsqrt(jnp.mean(shaped * shaped, axis=-1, keepdims=True) + 1e-05)
    return ((shaped * inv_rms).reshape(gated_rows.shape) * scales).astype(jnp.bfloat16)


def local(
    x_long,
    bc_long,
    z_long,
    dt_long,
    x_short,
    bc_short,
    z_short,
    dt_short,
    lengths,
    conv_x,
    conv_bc,
    conv_bias_x,
    conv_bias_bc,
    dt_bias,
    a_log,
    d_skip,
    norm_gain,
    out_weight,
    final_gain,
    head_weight,
):
    tok_rows, inner_cols = x_long.shape
    head_count = dt_long.shape[0]
    req_count = lengths.shape[0]
    rim_rows = KCONV - 1
    decay_rate = -jnp.exp(a_log)
    rim_x, rim_bc = passed_along(
        (x_long[tok_rows - rim_rows :], bc_long[tok_rows - rim_rows :]), "seq", 1
    )
    x_act = conv_act(jnp.concatenate([rim_x, x_long], 0), conv_x, conv_bias_x, tok_rows)
    bc_act = conv_act(jnp.concatenate([rim_bc, bc_long], 0), conv_bc, conv_bias_bc, tok_rows)
    dt_full = jax.nn.softplus(dt_long.astype(jnp.float32) + dt_bias[:, None])
    block_count = tok_rows // BLOCK
    x_blocks = x_act.reshape(block_count, BLOCK, head_count, HEADDIM)
    b_blocks = expand(bc_act[:, 0]).reshape(block_count, BLOCK, head_count, STATE)
    c_all = expand(bc_act[:, 1])
    c_blocks = c_all.reshape(block_count, BLOCK, head_count, STATE)
    dt_blocks = dt_full.reshape(head_count, block_count, BLOCK).transpose(1, 0, 2)

    start_state = jnp.zeros((head_count, HEADDIM, STATE), jnp.float32)
    local_state = start_state
    y_parts = []
    for index in range(block_count):
        y_block, local_state = ssd_block(
            x_blocks[index], b_blocks[index], c_blocks[index], dt_blocks[index], decay_rate, local_state
        )
        y_parts.append(y_block)
    y_blocks = jnp.stack(y_parts)
    cum_device = jnp.cumsum(dt_full * decay_rate[:, None], axis=1)
    total_log = cum_device[:, -1]
    carry_in = carry_scan(total_log, local_state, "seq")
    carried = jnp.exp(cum_device).T[:, :, None] * jnp.einsum(
        "thn,hpn->thp", c_all.astype(jnp.float32), carry_in, precision=lax.Precision.HIGHEST
    )
    y_long = (
        y_blocks.reshape(tok_rows, head_count, HEADDIM)
        + carried
        + d_skip[None, :, None] * x_act.reshape(tok_rows, head_count, HEADDIM).astype(jnp.float32)
    )
    block_states = (jnp.exp(total_log)[:, None, None] * carry_in + local_state)[None]
    normed_long = gate_norm(y_long.reshape(tok_rows, inner_cols), z_long, norm_gain)
    is_valid = jnp.arange(SLEN)[None, :] < lengths[:, None]
    zero_x = jnp.zeros((req_count, rim_rows) + x_short.shape[2:], jnp.bfloat16)
    zero_bc = jnp.zeros((req_count, rim_rows) + bc_short.shape[2:], jnp.bfloat16)
    x_sact = jax.vmap(lambda item: conv_act(item, conv_x, conv_bias_x, SLEN))(
        jnp.concatenate([zero_x, x_short], 1)
    )
    bc_sact = jax.vmap(lambda item: conv_act(item, conv_bc, conv_bias_bc, SLEN))(
        jnp.concatenate([zero_bc, bc_short], 1)
    )
    dt_sfull = jax.nn.softplus(dt_short.astype(jnp.float32) + dt_bias[:, None, None]) * is_valid[
        None
    ].astype(jnp.float32)
    dt_sfull = dt_sfull.transpose(1, 0, 2)

    def per_request(x_req, bc_req, dt_req):
        return ssd_block(
            x_req.reshape(SLEN, head_count, HEADDIM),
            expand(bc_req[:, 0]),
            expand(bc_req[:, 1]),
            dt_req,
            decay_rate,
            start_state,
        )

    y_sblocks, short_states = jax.vmap(per_request)(x_sact, bc_sact, dt_sfull)
    y_short = y_sblocks + d_skip[None, None, :, None] * x_sact.reshape(
        req_count, SLEN, head_count, HEADDIM
    ).astype(jnp.float32)
    normed_short = gate_norm(
        y_short.reshape(req_count * SLEN, inner_cols),
        z_short.reshape(req_count * SLEN, inner_cols),
        norm_gain,
    )
    tail_pick = (
        jnp.arange(SLEN)[None, None, :]
        == (lengths[:, None] - rim_rows + jnp.arange(rim_rows)[None, :])[:, :, None]
    ).astype(jnp.float32)
    tails_x = jnp.einsum(
        "rks,rsc->rkc", tail_pick, x_short.astype(jnp.float32), precision=lax.Precision.HIGHEST
    ).astype(jnp.bfloat16)
    tails_bc = jnp.einsum(
        "rks,rsbc->rkbc", tail_pick, bc_short.astype(jnp.float32), precision=lax.Precision.HIGHEST
    ).astype(jnp.bfloat16)
    all_normed = jnp.concatenate([normed_long, normed_short], 0)
    last_pick = (jnp.arange(SLEN)[None, :] == lengths[:, None] - 1).astype(jnp.float32)
    short_last = jnp.einsum(
        "rs,rsc->rc",
        last_pick,
        normed_short.reshape(req_count, SLEN, inner_cols).astype(jnp.float32),
        precision=lax.Precision.HIGHEST,
    ).astype(jnp.bfloat16)
    y_last = (
        y_blocks[-1, BLOCK - 1]
        + jnp.exp(total_log)[:, None]
        * jnp.einsum(
            "hn,hpn->hp",
            c_all[tok_rows - 1].astype(jnp.float32),
            carry_in,
            precision=lax.Precision.HIGHEST,
        )
        + d_skip[:, None] * x_act[tok_rows - 1].reshape(head_count, HEADDIM).astype(jnp.float32)
    )
    normed_last = gate_norm(y_last.reshape(1, inner_cols), z_long[tok_rows - 1 :], norm_gain)
    rows = tp_rows(jnp.concatenate([short_last, normed_last], 0), out_weight)
    seq_count = lax.axis_size("seq")
    shaped = gather_fast(rows, "seq", 0).reshape(seq_count, req_count + 1, D)
    long_row = shaped[seq_count - 1, req_count][None]
    short_all = shaped[:, :req_count].reshape(seq_count * req_count, D)
    last_norm = row_norm(jnp.concatenate([long_row, short_all], 0), final_gain)
    logits = lax.dot_general(
        last_norm, head_weight, (((1,), (1,)), ((), ())), preferred_element_type=jnp.float32
    )
    top_logit = max_fast(max_fast(jnp.max(logits, axis=1), "tp"), "seq")
    tp_count = lax.axis_size("tp")
    tp_index = lax.axis_index("tp")
    width = out_weight.shape[1] // tp_count
    total = None
    for step in (2, 1, 3, 0):
        if step >= tp_count:
            continue
        target = (tp_index + step) % tp_count
        piece = lax.dynamic_slice_in_dim(out_weight, target * width, width, 1)
        term = jnp.dot(all_normed, piece, preferred_element_type=jnp.float32).astype(jnp.bfloat16)
        if step:
            term, _ = lax.optimization_barrier((term, top_logit))
            term = lax.ppermute(
                term, "tp", [(i, (i + step) % tp_count) for i in range(tp_count)]
            )
        total = term.astype(jnp.float32) if total is None else total + term.astype(jnp.float32)
    hidden = total.astype(jnp.bfloat16)
    hidden_long = hidden[:tok_rows]
    hidden_short = hidden[tok_rows:].reshape(req_count, SLEN, -1) * is_valid[:, :, None].astype(
        jnp.bfloat16
    )
    return (
        hidden_long,
        hidden_short,
        block_states,
        short_states,
        tails_x,
        tails_bc,
        last_norm,
        top_logit,
    )


def solution(mesh):
    in_specs = (
        P("seq", "tp"),
        P("seq", None, "tp"),
        P("seq", "tp"),
        P("tp", "seq"),
        P("seq", None, "tp"),
        P("seq", None, None, "tp"),
        P("seq", None, "tp"),
        P("tp", "seq", None),
        P("seq"),
        P(None, "tp"),
        P(None, None, "tp"),
        P("tp"),
        P(None, "tp"),
        P("tp"),
        P("tp"),
        P("tp"),
        P("tp"),
        P("tp", None),
        P(),
        P(("seq", "tp"), None),
    )
    out_specs = (
        P("seq", "tp"),
        P("seq", None, "tp"),
        P("seq", "tp", None, None),
        P("seq", "tp", None, None),
        P("seq", None, "tp"),
        P("seq", None, None, "tp"),
        P(),
        P(),
    )
    return jax.shard_map(local, mesh=mesh, in_specs=in_specs, out_specs=out_specs, check_vma=False)
```

```python
import jax
import jax.numpy as jnp
from jax import lax
from jax.sharding import PartitionSpec as P

D = 4096
HEAD_SHARE = 64
HEADDIM = 64
GROUPS = 4
STATE = 128
KCONV = 4
BLOCK = 256
SLEN = 16


def passed_along(block, axis, distance):
    devices = range(lax.axis_size(axis))
    route = [(i - distance, i) for i in devices if i - distance in devices]
    return lax.ppermute(block, axis, route)


def swapped(block, axis, distance):
    devices = range(lax.axis_size(axis))
    return lax.ppermute(block, axis, [(i, i ^ distance) for i in devices])


def gather_all(block, axis, dim):
    count = lax.axis_size(axis)
    index = lax.axis_index(axis)
    distance = 1
    while distance < count:
        other = swapped(block, axis, distance)
        low = (index // distance) % 2 == 0
        block = jnp.where(
            low, jnp.concatenate([block, other], dim), jnp.concatenate([other, block], dim)
        )
        distance *= 2
    return block


def max_all(block, axis):
    distance = 1
    while distance < lax.axis_size(axis):
        block = jnp.maximum(block, swapped(block, axis, distance))
        distance *= 2
    return block


def digit_route(count, distance, step, radix):
    route = []
    for i in range(count):
        digit = (i // distance) % radix
        route.append((i, i + ((digit + step) % radix - digit) * distance))
    return route


def gather_fast(block, axis, dim):
    count = lax.axis_size(axis)
    index = lax.axis_index(axis)
    distance = 1
    while distance < count:
        radix = min(4, count // distance)
        digit = (index // distance) % radix
        got = [block] + [
            lax.ppermute(block, axis, digit_route(count, distance, step, radix))
            for step in range(1, radix)
        ]
        stacked = jnp.stack(got)
        parts = [
            lax.dynamic_index_in_dim(stacked, (digit - part) % radix, 0, keepdims=False)
            for part in range(radix)
        ]
        block = jnp.concatenate(parts, dim)
        distance *= radix
    return block


def max_fast(block, axis):
    count = lax.axis_size(axis)
    distance = 1
    while distance < count:
        radix = min(4, count // distance)
        got = [
            lax.ppermute(block, axis, digit_route(count, distance, step, radix))
            for step in range(1, radix)
        ]
        for other in got:
            block = jnp.maximum(block, other)
        distance *= radix
    return block


def pack(state, log):
    heads = log.shape[0]
    high = log.astype(jnp.bfloat16)
    rest = log - high.astype(jnp.float32)
    mid = rest.astype(jnp.bfloat16)
    low = (rest - mid.astype(jnp.float32)).astype(jnp.bfloat16)
    lanes = state.shape[-1]
    row = jnp.concatenate([high, mid, low, jnp.zeros((lanes - 3 * heads,), jnp.bfloat16)])
    flat = state.astype(jnp.bfloat16).reshape(-1, lanes)
    return jnp.concatenate([flat, row[None]], 0)


def unpack(message, heads):
    lanes = message.shape[-1]
    state = message[:-1].reshape(heads, -1, lanes).astype(jnp.float32)
    row = message[-1].astype(jnp.float32)
    log = (row[:heads] + row[heads : 2 * heads]) + row[2 * heads : 3 * heads]
    return log, state


def carry_scan(total_log, local_state, axis):
    heads = total_log.shape[0]
    sent = pack(local_state, total_log)
    log_one, state_one = unpack(passed_along(sent, axis, 1), heads)
    log_two, state_two = unpack(passed_along(sent, axis, 2), heads)
    seg_log = log_one + log_two
    seg_state = jnp.exp(log_one)[:, None, None] * state_two + state_one
    distance = 2
    while distance < lax.axis_size(axis):
        got_log, got_state = unpack(passed_along(pack(seg_state, seg_log), axis, distance), heads)
        seg_state = jnp.exp(seg_log)[:, None, None] * got_state + seg_state
        seg_log = seg_log + got_log
        distance *= 2
    return seg_state


def conv_act(padded, weight, shift_bias, span_len):
    running_sum = shift_bias + 0.0 * padded[:span_len].astype(jnp.float32)
    for offset in range(weight.shape[0]):
        running_sum = running_sum + weight[offset] * padded[offset : offset + span_len].astype(
            jnp.float32
        )
    return jax.nn.silu(running_sum).astype(jnp.bfloat16)


def expand(portion):
    shaped = portion.reshape(portion.shape[:-1] + (portion.shape[-1] // STATE, STATE))
    return jnp.repeat(shaped, HEAD_SHARE // GROUPS, axis=-2)


def ssd_block(x_block, b_block, c_block, dt_block, decay_rate, state_in):
    step_log = dt_block * decay_rate[:, None]
    cumulative = jnp.cumsum(step_log, axis=1)
    span_len = x_block.shape[0]
    positions = jnp.arange(span_len)
    causal = (positions[:, None] >= positions[None, :])[None]
    log_gap = jnp.where(causal, cumulative[:, :, None] - cumulative[:, None, :], 0.0)
    decay_table = jnp.where(causal, jnp.exp(log_gap), 0.0)
    scores = jnp.einsum("thn,shn->hts", c_block, b_block, preferred_element_type=jnp.float32)
    weights = (scores * decay_table * dt_block[:, None, :]).astype(jnp.bfloat16)
    y_intra = jnp.einsum("hts,shp->thp", weights, x_block, preferred_element_type=jnp.float32)
    y_state = jnp.exp(cumulative).T[:, :, None] * jnp.einsum(
        "thn,hpn->thp", c_block.astype(jnp.float32), state_in, precision=lax.Precision.HIGHEST
    )
    to_end = jnp.exp(cumulative[:, -1:] - cumulative) * dt_block
    scaled = (x_block.astype(jnp.float32) * to_end.T[:, :, None]).astype(jnp.bfloat16)
    next_state = jnp.exp(cumulative[:, -1])[:, None, None] * state_in + jnp.einsum(
        "shp,shn->hpn", scaled, b_block, preferred_element_type=jnp.float32
    )
    return (y_intra + y_state, next_state)


def gate_norm(values, gating, scales):
    gated_rows = values * jax.nn.silu(gating.astype(jnp.float32))
    size_group = HEAD_SHARE // GROUPS * HEADDIM
    shaped = gated_rows.reshape(gated_rows.shape[0], -1, size_group)
    inv_rms = lax.rsqrt(jnp.mean(shaped * shaped, axis=-1, keepdims=True) + 1e-05)
    return ((shaped * inv_rms).reshape(gated_rows.shape) * scales).astype(jnp.bfloat16)


def local(
    x_long,
    bc_long,
    z_long,
    dt_long,
    x_short,
    bc_short,
    z_short,
    dt_short,
    lengths,
    conv_x,
    conv_bc,
    conv_bias_x,
    conv_bias_bc,
    dt_bias,
    a_log,
    d_skip,
    norm_gain,
    out_weight,
    final_gain,
    head_weight,
):
    tok_rows, inner_cols = x_long.shape
    head_count = dt_long.shape[0]
    req_count = lengths.shape[0]
    rim_rows = KCONV - 1
    decay_rate = -jnp.exp(a_log)
    rim_x, rim_bc = passed_along(
        (x_long[tok_rows - rim_rows :], bc_long[tok_rows - rim_rows :]), "seq", 1
    )
    x_act = conv_act(jnp.concatenate([rim_x, x_long], 0), conv_x, conv_bias_x, tok_rows)
    bc_act = conv_act(jnp.concatenate([rim_bc, bc_long], 0), conv_bc, conv_bias_bc, tok_rows)
    dt_full = jax.nn.softplus(dt_long.astype(jnp.float32) + dt_bias[:, None])
    block_count = tok_rows // BLOCK
    x_blocks = x_act.reshape(block_count, BLOCK, head_count, HEADDIM)
    b_blocks = expand(bc_act[:, 0]).reshape(block_count, BLOCK, head_count, STATE)
    c_all = expand(bc_act[:, 1])
    c_blocks = c_all.reshape(block_count, BLOCK, head_count, STATE)
    dt_blocks = dt_full.reshape(head_count, block_count, BLOCK).transpose(1, 0, 2)

    start_state = jnp.zeros((head_count, HEADDIM, STATE), jnp.float32)
    local_state = start_state
    y_parts = []
    for index in range(block_count):
        y_block, local_state = ssd_block(
            x_blocks[index], b_blocks[index], c_blocks[index], dt_blocks[index], decay_rate, local_state
        )
        y_parts.append(y_block)
    y_blocks = jnp.stack(y_parts)
    cum_device = jnp.cumsum(dt_full * decay_rate[:, None], axis=1)
    total_log = cum_device[:, -1]
    carry_in = carry_scan(total_log, local_state, "seq")
    carried = jnp.exp(cum_device).T[:, :, None] * jnp.einsum(
        "thn,hpn->thp", c_all.astype(jnp.float32), carry_in, precision=lax.Precision.HIGHEST
    )
    y_long = (
        y_blocks.reshape(tok_rows, head_count, HEADDIM)
        + carried
        + d_skip[None, :, None] * x_act.reshape(tok_rows, head_count, HEADDIM).astype(jnp.float32)
    )
    block_states = (jnp.exp(total_log)[:, None, None] * carry_in + local_state)[None]
    normed_long = gate_norm(y_long.reshape(tok_rows, inner_cols), z_long, norm_gain)
    is_valid = jnp.arange(SLEN)[None, :] < lengths[:, None]
    zero_x = jnp.zeros((req_count, rim_rows) + x_short.shape[2:], jnp.bfloat16)
    zero_bc = jnp.zeros((req_count, rim_rows) + bc_short.shape[2:], jnp.bfloat16)
    x_sact = jax.vmap(lambda item: conv_act(item, conv_x, conv_bias_x, SLEN))(
        jnp.concatenate([zero_x, x_short], 1)
    )
    bc_sact = jax.vmap(lambda item: conv_act(item, conv_bc, conv_bias_bc, SLEN))(
        jnp.concatenate([zero_bc, bc_short], 1)
    )
    dt_sfull = jax.nn.softplus(dt_short.astype(jnp.float32) + dt_bias[:, None, None]) * is_valid[
        None
    ].astype(jnp.float32)
    dt_sfull = dt_sfull.transpose(1, 0, 2)

    def per_request(x_req, bc_req, dt_req):
        return ssd_block(
            x_req.reshape(SLEN, head_count, HEADDIM),
            expand(bc_req[:, 0]),
            expand(bc_req[:, 1]),
            dt_req,
            decay_rate,
            start_state,
        )

    y_sblocks, short_states = jax.vmap(per_request)(x_sact, bc_sact, dt_sfull)
    y_short = y_sblocks + d_skip[None, None, :, None] * x_sact.reshape(
        req_count, SLEN, head_count, HEADDIM
    ).astype(jnp.float32)
    normed_short = gate_norm(
        y_short.reshape(req_count * SLEN, inner_cols),
        z_short.reshape(req_count * SLEN, inner_cols),
        norm_gain,
    )
    tail_pick = (
        jnp.arange(SLEN)[None, None, :]
        == (lengths[:, None] - rim_rows + jnp.arange(rim_rows)[None, :])[:, :, None]
    ).astype(jnp.float32)
    tails_x = jnp.einsum(
        "rks,rsc->rkc", tail_pick, x_short.astype(jnp.float32), precision=lax.Precision.HIGHEST
    ).astype(jnp.bfloat16)
    tails_bc = jnp.einsum(
        "rks,rsbc->rkbc", tail_pick, bc_short.astype(jnp.float32), precision=lax.Precision.HIGHEST
    ).astype(jnp.bfloat16)
    all_normed = jnp.concatenate([normed_long, normed_short], 0)
    tp_count = lax.axis_size("tp")
    tp_index = lax.axis_index("tp")
    width = out_weight.shape[1] // tp_count
    out_terms = jnp.dot(all_normed, out_weight, preferred_element_type=jnp.float32).astype(
        jnp.bfloat16
    )
    last_pick = (jnp.arange(SLEN)[None, :] == lengths[:, None] - 1).astype(jnp.float32)
    total = None
    row_total = None
    for step in (2, 1, 3, 0):
        if step >= tp_count:
            continue
        target = (tp_index + step) % tp_count
        term = lax.dynamic_slice_in_dim(out_terms, target * width, width, 1)
        if step:
            term = lax.ppermute(
                term, "tp", [(i, (i + step) % tp_count) for i in range(tp_count)]
            )
        picked = jnp.concatenate(
            [
                jnp.einsum(
                    "rs,rsd->rd",
                    last_pick,
                    term[tok_rows:].reshape(req_count, SLEN, -1).astype(jnp.float32),
                    precision=lax.Precision.HIGHEST,
                ),
                term[tok_rows - 1 : tok_rows].astype(jnp.float32),
            ],
            0,
        )
        total = term.astype(jnp.float32) if total is None else total + term.astype(jnp.float32)
        row_total = picked if row_total is None else row_total + picked
    hidden = total.astype(jnp.bfloat16)
    hidden_long = hidden[:tok_rows]
    hidden_short = hidden[tok_rows:].reshape(req_count, SLEN, -1) * is_valid[:, :, None].astype(
        jnp.bfloat16
    )
    packed = row_total.astype(jnp.bfloat16)
    seq_rows = gather_fast(packed, "seq", 0)
    full_rows = gather_fast(seq_rows, "tp", 1)
    seq_count = lax.axis_size("seq")
    shaped = full_rows.reshape(seq_count, req_count + 1, D)
    long_row = shaped[seq_count - 1, req_count][None]
    short_all = shaped[:, :req_count].reshape(seq_count * req_count, D)
    row_block = jnp.concatenate([long_row, short_all], 0).astype(jnp.float32)
    last_norm = (
        row_block
        * lax.rsqrt(jnp.mean(row_block * row_block, axis=-1, keepdims=True) + 1e-05)
        * final_gain
    ).astype(jnp.bfloat16)
    logits = lax.dot_general(
        last_norm, head_weight, (((1,), (1,)), ((), ())), preferred_element_type=jnp.float32
    )
    top_logit = max_fast(max_fast(jnp.max(logits, axis=1), "tp"), "seq")
    return (
        hidden_long,
        hidden_short,
        block_states,
        short_states,
        tails_x,
        tails_bc,
        last_norm,
        top_logit,
    )


def solution(mesh):
    in_specs = (
        P("seq", "tp"),
        P("seq", None, "tp"),
        P("seq", "tp"),
        P("tp", "seq"),
        P("seq", None, "tp"),
        P("seq", None, None, "tp"),
        P("seq", None, "tp"),
        P("tp", "seq", None),
        P("seq"),
        P(None, "tp"),
        P(None, None, "tp"),
        P("tp"),
        P(None, "tp"),
        P("tp"),
        P("tp"),
        P("tp"),
        P("tp"),
        P("tp", None),
        P(),
        P(("seq", "tp"), None),
    )
    out_specs = (
        P("seq", "tp"),
        P("seq", None, "tp"),
        P("seq", "tp", None, None),
        P("seq", "tp", None, None),
        P("seq", None, "tp"),
        P("seq", None, None, "tp"),
        P(),
        P(),
    )
    return jax.shard_map(local, mesh=mesh, in_specs=in_specs, out_specs=out_specs, check_vma=False)
```

```python
import jax
import jax.numpy as jnp
from jax import lax
from jax.sharding import PartitionSpec as P

D = 4096
HEAD_SHARE = 64
HEADDIM = 64
GROUPS = 4
STATE = 128
KCONV = 4
BLOCK = 256
SLEN = 16


def passed_along(block, axis, distance):
    devices = range(lax.axis_size(axis))
    route = [(i - distance, i) for i in devices if i - distance in devices]
    return lax.ppermute(block, axis, route)


def swapped(block, axis, distance):
    devices = range(lax.axis_size(axis))
    return lax.ppermute(block, axis, [(i, i ^ distance) for i in devices])


def gather_all(block, axis, dim):
    count = lax.axis_size(axis)
    index = lax.axis_index(axis)
    distance = 1
    while distance < count:
        other = swapped(block, axis, distance)
        low = (index // distance) % 2 == 0
        block = jnp.where(
            low, jnp.concatenate([block, other], dim), jnp.concatenate([other, block], dim)
        )
        distance *= 2
    return block


def max_all(block, axis):
    distance = 1
    while distance < lax.axis_size(axis):
        block = jnp.maximum(block, swapped(block, axis, distance))
        distance *= 2
    return block


def digit_route(count, distance, step, radix):
    route = []
    for i in range(count):
        digit = (i // distance) % radix
        route.append((i, i + ((digit + step) % radix - digit) * distance))
    return route


def gather_fast(block, axis, dim):
    count = lax.axis_size(axis)
    index = lax.axis_index(axis)
    distance = 1
    while distance < count:
        radix = min(4, count // distance)
        digit = (index // distance) % radix
        got = [block] + [
            lax.ppermute(block, axis, digit_route(count, distance, step, radix))
            for step in range(1, radix)
        ]
        stacked = jnp.stack(got)
        parts = [
            lax.dynamic_index_in_dim(stacked, (digit - part) % radix, 0, keepdims=False)
            for part in range(radix)
        ]
        block = jnp.concatenate(parts, dim)
        distance *= radix
    return block


def max_fast(block, axis):
    count = lax.axis_size(axis)
    distance = 1
    while distance < count:
        radix = min(4, count // distance)
        got = [
            lax.ppermute(block, axis, digit_route(count, distance, step, radix))
            for step in range(1, radix)
        ]
        for other in got:
            block = jnp.maximum(block, other)
        distance *= radix
    return block


def carry_scan(total_log, local_state, axis):
    sent = local_state.astype(jnp.bfloat16)
    log_one, state_one = passed_along((total_log, sent), axis, 1)
    log_two, state_two = passed_along((total_log, sent), axis, 2)
    seg_log = log_one + log_two
    seg_state = jnp.exp(log_one)[:, None, None] * state_two.astype(jnp.float32) + state_one.astype(
        jnp.float32
    )
    distance = 2
    while distance < lax.axis_size(axis):
        got_log, got_state = passed_along(
            (seg_log, seg_state.astype(jnp.bfloat16)), axis, distance
        )
        seg_state = jnp.exp(seg_log)[:, None, None] * got_state.astype(jnp.float32) + seg_state
        seg_log = seg_log + got_log
        distance *= 2
    return seg_state


def conv_act(padded, weight, shift_bias, span_len):
    running_sum = shift_bias + 0.0 * padded[:span_len].astype(jnp.float32)
    for offset in range(weight.shape[0]):
        running_sum = running_sum + weight[offset] * padded[offset : offset + span_len].astype(
            jnp.float32
        )
    return jax.nn.silu(running_sum).astype(jnp.bfloat16)


def expand(portion):
    shaped = portion.reshape(portion.shape[:-1] + (portion.shape[-1] // STATE, STATE))
    return jnp.repeat(shaped, HEAD_SHARE // GROUPS, axis=-2)


def ssd_block(x_block, b_block, c_block, dt_block, decay_rate, state_in):
    step_log = dt_block * decay_rate[:, None]
    cumulative = jnp.cumsum(step_log, axis=1)
    span_len = x_block.shape[0]
    positions = jnp.arange(span_len)
    causal = (positions[:, None] >= positions[None, :])[None]
    log_gap = jnp.where(causal, cumulative[:, :, None] - cumulative[:, None, :], 0.0)
    decay_table = jnp.where(causal, jnp.exp(log_gap), 0.0)
    scores = jnp.einsum("thn,shn->hts", c_block, b_block, preferred_element_type=jnp.float32)
    weights = (scores * decay_table * dt_block[:, None, :]).astype(jnp.bfloat16)
    y_intra = jnp.einsum("hts,shp->thp", weights, x_block, preferred_element_type=jnp.float32)
    y_state = jnp.exp(cumulative).T[:, :, None] * jnp.einsum(
        "thn,hpn->thp", c_block.astype(jnp.float32), state_in, precision=lax.Precision.HIGHEST
    )
    to_end = jnp.exp(cumulative[:, -1:] - cumulative) * dt_block
    scaled = (x_block.astype(jnp.float32) * to_end.T[:, :, None]).astype(jnp.bfloat16)
    next_state = jnp.exp(cumulative[:, -1])[:, None, None] * state_in + jnp.einsum(
        "shp,shn->hpn", scaled, b_block, preferred_element_type=jnp.float32
    )
    return (y_intra + y_state, next_state)


def gate_norm(values, gating, scales):
    gated_rows = values * jax.nn.silu(gating.astype(jnp.float32))
    size_group = HEAD_SHARE // GROUPS * HEADDIM
    shaped = gated_rows.reshape(gated_rows.shape[0], -1, size_group)
    inv_rms = lax.rsqrt(jnp.mean(shaped * shaped, axis=-1, keepdims=True) + 1e-05)
    return ((shaped * inv_rms).reshape(gated_rows.shape) * scales).astype(jnp.bfloat16)


def local(
    x_long,
    bc_long,
    z_long,
    dt_long,
    x_short,
    bc_short,
    z_short,
    dt_short,
    lengths,
    conv_x,
    conv_bc,
    conv_bias_x,
    conv_bias_bc,
    dt_bias,
    a_log,
    d_skip,
    norm_gain,
    out_weight,
    final_gain,
    head_weight,
):
    tok_rows, inner_cols = x_long.shape
    head_count = dt_long.shape[0]
    req_count = lengths.shape[0]
    rim_rows = KCONV - 1
    decay_rate = -jnp.exp(a_log)
    rim_x, rim_bc = passed_along(
        (x_long[tok_rows - rim_rows :], bc_long[tok_rows - rim_rows :]), "seq", 1
    )
    x_act = conv_act(jnp.concatenate([rim_x, x_long], 0), conv_x, conv_bias_x, tok_rows)
    bc_act = conv_act(jnp.concatenate([rim_bc, bc_long], 0), conv_bc, conv_bias_bc, tok_rows)
    dt_full = jax.nn.softplus(dt_long.astype(jnp.float32) + dt_bias[:, None])
    block_count = tok_rows // BLOCK
    x_blocks = x_act.reshape(block_count, BLOCK, head_count, HEADDIM)
    b_blocks = expand(bc_act[:, 0]).reshape(block_count, BLOCK, head_count, STATE)
    c_all = expand(bc_act[:, 1])
    c_blocks = c_all.reshape(block_count, BLOCK, head_count, STATE)
    dt_blocks = dt_full.reshape(head_count, block_count, BLOCK).transpose(1, 0, 2)

    start_state = jnp.zeros((head_count, HEADDIM, STATE), jnp.float32)
    local_state = start_state
    y_parts = []
    for index in range(block_count):
        y_block, local_state = ssd_block(
            x_blocks[index], b_blocks[index], c_blocks[index], dt_blocks[index], decay_rate, local_state
        )
        y_parts.append(y_block)
    y_blocks = jnp.stack(y_parts)
    cum_device = jnp.cumsum(dt_full * decay_rate[:, None], axis=1)
    total_log = cum_device[:, -1]
    carry_in = carry_scan(total_log, local_state, "seq")
    carried = jnp.exp(cum_device).T[:, :, None] * jnp.einsum(
        "thn,hpn->thp", c_all.astype(jnp.float32), carry_in, precision=lax.Precision.HIGHEST
    )
    y_long = (
        y_blocks.reshape(tok_rows, head_count, HEADDIM)
        + carried
        + d_skip[None, :, None] * x_act.reshape(tok_rows, head_count, HEADDIM).astype(jnp.float32)
    )
    block_states = (jnp.exp(total_log)[:, None, None] * carry_in + local_state)[None]
    normed_long = gate_norm(y_long.reshape(tok_rows, inner_cols), z_long, norm_gain)
    is_valid = jnp.arange(SLEN)[None, :] < lengths[:, None]
    zero_x = jnp.zeros((req_count, rim_rows) + x_short.shape[2:], jnp.bfloat16)
    zero_bc = jnp.zeros((req_count, rim_rows) + bc_short.shape[2:], jnp.bfloat16)
    x_sact = jax.vmap(lambda item: conv_act(item, conv_x, conv_bias_x, SLEN))(
        jnp.concatenate([zero_x, x_short], 1)
    )
    bc_sact = jax.vmap(lambda item: conv_act(item, conv_bc, conv_bias_bc, SLEN))(
        jnp.concatenate([zero_bc, bc_short], 1)
    )
    dt_sfull = jax.nn.softplus(dt_short.astype(jnp.float32) + dt_bias[:, None, None]) * is_valid[
        None
    ].astype(jnp.float32)
    dt_sfull = dt_sfull.transpose(1, 0, 2)

    def per_request(x_req, bc_req, dt_req):
        return ssd_block(
            x_req.reshape(SLEN, head_count, HEADDIM),
            expand(bc_req[:, 0]),
            expand(bc_req[:, 1]),
            dt_req,
            decay_rate,
            start_state,
        )

    y_sblocks, short_states = jax.vmap(per_request)(x_sact, bc_sact, dt_sfull)
    y_short = y_sblocks + d_skip[None, None, :, None] * x_sact.reshape(
        req_count, SLEN, head_count, HEADDIM
    ).astype(jnp.float32)
    normed_short = gate_norm(
        y_short.reshape(req_count * SLEN, inner_cols),
        z_short.reshape(req_count * SLEN, inner_cols),
        norm_gain,
    )
    tail_pick = (
        jnp.arange(SLEN)[None, None, :]
        == (lengths[:, None] - rim_rows + jnp.arange(rim_rows)[None, :])[:, :, None]
    ).astype(jnp.float32)
    tails_x = jnp.einsum(
        "rks,rsc->rkc", tail_pick, x_short.astype(jnp.float32), precision=lax.Precision.HIGHEST
    ).astype(jnp.bfloat16)
    tails_bc = jnp.einsum(
        "rks,rsbc->rkbc", tail_pick, bc_short.astype(jnp.float32), precision=lax.Precision.HIGHEST
    ).astype(jnp.bfloat16)
    all_normed = jnp.concatenate([normed_long, normed_short], 0)
    tp_count = lax.axis_size("tp")
    tp_index = lax.axis_index("tp")
    width = out_weight.shape[1] // tp_count
    blocks = []
    for step in range(tp_count):
        target = (tp_index + step) % tp_count
        piece = lax.dynamic_slice_in_dim(out_weight, target * width, width, 1)
        blocks.append(
            jnp.dot(all_normed, piece, preferred_element_type=jnp.float32).astype(jnp.bfloat16)
        )
    rows_all = all_normed.shape[0]
    half = rows_all // 2
    ahead = [(i, (i + 1) % tp_count) for i in range(tp_count)]
    behind = [(i, (i + tp_count - 1) % tp_count) for i in range(tp_count)]
    from_prev = lax.ppermute(jnp.concatenate([blocks[1], blocks[2][:half]], 0), "tp", ahead)
    from_next = lax.ppermute(jnp.concatenate([blocks[3], blocks[2][half:]], 0), "tp", behind)
    far_top = lax.ppermute(from_prev[rows_all:], "tp", ahead)
    far_bottom = lax.ppermute(from_next[rows_all:], "tp", behind)
    far = jnp.concatenate([far_top, far_bottom], 0)
    total = far.astype(jnp.float32)
    total = total + from_prev[:rows_all].astype(jnp.float32)
    total = total + from_next[:rows_all].astype(jnp.float32)
    total = total + blocks[0].astype(jnp.float32)
    hidden = total.astype(jnp.bfloat16)
    hidden_long = hidden[:tok_rows]
    hidden_short = hidden[tok_rows:].reshape(req_count, SLEN, -1) * is_valid[:, :, None].astype(
        jnp.bfloat16
    )
    last_pick = (jnp.arange(SLEN)[None, :] == lengths[:, None] - 1).astype(jnp.float32)
    short_rows = jnp.einsum(
        "rs,rsd->rd", last_pick, hidden_short.astype(jnp.float32), precision=lax.Precision.HIGHEST
    ).astype(jnp.bfloat16)
    packed = jnp.concatenate([short_rows, hidden_long[tok_rows - 1 :]], 0)
    seq_rows = gather_fast(packed, "seq", 0)
    full_rows = gather_fast(seq_rows, "tp", 1)
    seq_count = lax.axis_size("seq")
    shaped = full_rows.reshape(seq_count, req_count + 1, D)
    long_row = shaped[seq_count - 1, req_count][None]
    short_all = shaped[:, :req_count].reshape(seq_count * req_count, D)
    row_block = jnp.concatenate([long_row, short_all], 0).astype(jnp.float32)
    last_norm = (
        row_block
        * lax.rsqrt(jnp.mean(row_block * row_block, axis=-1, keepdims=True) + 1e-05)
        * final_gain
    ).astype(jnp.bfloat16)
    logits = lax.dot_general(
        last_norm, head_weight, (((1,), (1,)), ((), ())), preferred_element_type=jnp.float32
    )
    top_logit = max_fast(max_fast(jnp.max(logits, axis=1), "tp"), "seq")
    return (
        hidden_long,
        hidden_short,
        block_states,
        short_states,
        tails_x,
        tails_bc,
        last_norm,
        top_logit,
    )


def solution(mesh):
    in_specs = (
        P("seq", "tp"),
        P("seq", None, "tp"),
        P("seq", "tp"),
        P("tp", "seq"),
        P("seq", None, "tp"),
        P("seq", None, None, "tp"),
        P("seq", None, "tp"),
        P("tp", "seq", None),
        P("seq"),
        P(None, "tp"),
        P(None, None, "tp"),
        P("tp"),
        P(None, "tp"),
        P("tp"),
        P("tp"),
        P("tp"),
        P("tp"),
        P("tp", None),
        P(),
        P(("seq", "tp"), None),
    )
    out_specs = (
        P("seq", "tp"),
        P("seq", None, "tp"),
        P("seq", "tp", None, None),
        P("seq", "tp", None, None),
        P("seq", None, "tp"),
        P("seq", None, None, "tp"),
        P(),
        P(),
    )
    return jax.shard_map(local, mesh=mesh, in_specs=in_specs, out_specs=out_specs, check_vma=False)
```

```python
import jax
import jax.numpy as jnp
from jax import lax
from jax.sharding import PartitionSpec as P

D = 4096
HEAD_SHARE = 64
HEADDIM = 64
GROUPS = 4
STATE = 128
KCONV = 4
BLOCK = 256
SLEN = 16


def passed_along(block, axis, distance):
    devices = range(lax.axis_size(axis))
    route = [(i - distance, i) for i in devices if i - distance in devices]
    return lax.ppermute(block, axis, route)


def swapped(block, axis, distance):
    devices = range(lax.axis_size(axis))
    return lax.ppermute(block, axis, [(i, i ^ distance) for i in devices])


def gather_all(block, axis, dim):
    count = lax.axis_size(axis)
    index = lax.axis_index(axis)
    distance = 1
    while distance < count:
        other = swapped(block, axis, distance)
        low = (index // distance) % 2 == 0
        block = jnp.where(
            low, jnp.concatenate([block, other], dim), jnp.concatenate([other, block], dim)
        )
        distance *= 2
    return block


def max_all(block, axis):
    distance = 1
    while distance < lax.axis_size(axis):
        block = jnp.maximum(block, swapped(block, axis, distance))
        distance *= 2
    return block


def digit_route(count, distance, step, radix):
    route = []
    for i in range(count):
        digit = (i // distance) % radix
        route.append((i, i + ((digit + step) % radix - digit) * distance))
    return route


def gather_fast(block, axis, dim):
    count = lax.axis_size(axis)
    index = lax.axis_index(axis)
    distance = 1
    while distance < count:
        radix = min(4, count // distance)
        digit = (index // distance) % radix
        got = [block] + [
            lax.ppermute(block, axis, digit_route(count, distance, step, radix))
            for step in range(1, radix)
        ]
        stacked = jnp.stack(got)
        parts = [
            lax.dynamic_index_in_dim(stacked, (digit - part) % radix, 0, keepdims=False)
            for part in range(radix)
        ]
        block = jnp.concatenate(parts, dim)
        distance *= radix
    return block


def max_fast(block, axis):
    count = lax.axis_size(axis)
    distance = 1
    while distance < count:
        radix = min(4, count // distance)
        got = [
            lax.ppermute(block, axis, digit_route(count, distance, step, radix))
            for step in range(1, radix)
        ]
        for other in got:
            block = jnp.maximum(block, other)
        distance *= radix
    return block


def carry_scan(total_log, local_state, axis):
    sent = local_state.astype(jnp.bfloat16)
    log_one, state_one = passed_along((total_log, sent), axis, 1)
    log_two, state_two = passed_along((total_log, sent), axis, 2)
    seg_log = log_one + log_two
    seg_state = jnp.exp(log_one)[:, None, None] * state_two.astype(jnp.float32) + state_one.astype(
        jnp.float32
    )
    distance = 2
    while distance < lax.axis_size(axis):
        got_log, got_state = passed_along(
            (seg_log, seg_state.astype(jnp.bfloat16)), axis, distance
        )
        seg_state = jnp.exp(seg_log)[:, None, None] * got_state.astype(jnp.float32) + seg_state
        seg_log = seg_log + got_log
        distance *= 2
    return seg_state


def conv_act(padded, weight, shift_bias, span_len):
    running_sum = shift_bias + 0.0 * padded[:span_len].astype(jnp.float32)
    for offset in range(weight.shape[0]):
        running_sum = running_sum + weight[offset] * padded[offset : offset + span_len].astype(
            jnp.float32
        )
    return jax.nn.silu(running_sum).astype(jnp.bfloat16)


def expand(portion):
    shaped = portion.reshape(portion.shape[:-1] + (portion.shape[-1] // STATE, STATE))
    return jnp.repeat(shaped, HEAD_SHARE // GROUPS, axis=-2)


def ssd_block(x_block, b_block, c_block, dt_block, decay_rate, state_in):
    step_log = dt_block * decay_rate[:, None]
    cumulative = jnp.cumsum(step_log, axis=1)
    span_len = x_block.shape[0]
    positions = jnp.arange(span_len)
    causal = (positions[:, None] >= positions[None, :])[None]
    log_gap = jnp.where(causal, cumulative[:, :, None] - cumulative[:, None, :], 0.0)
    decay_table = jnp.where(causal, jnp.exp(log_gap), 0.0)
    scores = jnp.einsum("thn,shn->hts", c_block, b_block, preferred_element_type=jnp.float32)
    weights = (scores * decay_table * dt_block[:, None, :]).astype(jnp.bfloat16)
    y_intra = jnp.einsum("hts,shp->thp", weights, x_block, preferred_element_type=jnp.float32)
    y_state = jnp.exp(cumulative).T[:, :, None] * jnp.einsum(
        "thn,hpn->thp", c_block.astype(jnp.float32), state_in, precision=lax.Precision.HIGHEST
    )
    to_end = jnp.exp(cumulative[:, -1:] - cumulative) * dt_block
    scaled = (x_block.astype(jnp.float32) * to_end.T[:, :, None]).astype(jnp.bfloat16)
    next_state = jnp.exp(cumulative[:, -1])[:, None, None] * state_in + jnp.einsum(
        "shp,shn->hpn", scaled, b_block, preferred_element_type=jnp.float32
    )
    return (y_intra + y_state, next_state)


def gate_norm(values, gating, scales):
    gated_rows = values * jax.nn.silu(gating.astype(jnp.float32))
    size_group = HEAD_SHARE // GROUPS * HEADDIM
    shaped = gated_rows.reshape(gated_rows.shape[0], -1, size_group)
    inv_rms = lax.rsqrt(jnp.mean(shaped * shaped, axis=-1, keepdims=True) + 1e-05)
    return ((shaped * inv_rms).reshape(gated_rows.shape) * scales).astype(jnp.bfloat16)


def local(
    x_long,
    bc_long,
    z_long,
    dt_long,
    x_short,
    bc_short,
    z_short,
    dt_short,
    lengths,
    conv_x,
    conv_bc,
    conv_bias_x,
    conv_bias_bc,
    dt_bias,
    a_log,
    d_skip,
    norm_gain,
    out_weight,
    final_gain,
    head_weight,
):
    tok_rows, inner_cols = x_long.shape
    head_count = dt_long.shape[0]
    req_count = lengths.shape[0]
    rim_rows = KCONV - 1
    decay_rate = -jnp.exp(a_log)
    rim_x, rim_bc = passed_along(
        (x_long[tok_rows - rim_rows :], bc_long[tok_rows - rim_rows :]), "seq", 1
    )
    x_act = conv_act(jnp.concatenate([rim_x, x_long], 0), conv_x, conv_bias_x, tok_rows)
    bc_act = conv_act(jnp.concatenate([rim_bc, bc_long], 0), conv_bc, conv_bias_bc, tok_rows)
    dt_full = jax.nn.softplus(dt_long.astype(jnp.float32) + dt_bias[:, None])
    block_count = tok_rows // BLOCK
    x_blocks = x_act.reshape(block_count, BLOCK, head_count, HEADDIM)
    b_blocks = expand(bc_act[:, 0]).reshape(block_count, BLOCK, head_count, STATE)
    c_all = expand(bc_act[:, 1])
    c_blocks = c_all.reshape(block_count, BLOCK, head_count, STATE)
    dt_blocks = dt_full.reshape(head_count, block_count, BLOCK).transpose(1, 0, 2)

    start_state = jnp.zeros((head_count, HEADDIM, STATE), jnp.float32)
    local_state = start_state
    y_parts = []
    for index in range(block_count):
        y_block, local_state = ssd_block(
            x_blocks[index], b_blocks[index], c_blocks[index], dt_blocks[index], decay_rate, local_state
        )
        y_parts.append(y_block)
    y_blocks = jnp.stack(y_parts)
    cum_device = jnp.cumsum(dt_full * decay_rate[:, None], axis=1)
    total_log = cum_device[:, -1]
    carry_in = carry_scan(total_log, local_state, "seq")
    carried = jnp.exp(cum_device).T[:, :, None] * jnp.einsum(
        "thn,hpn->thp", c_all.astype(jnp.float32), carry_in, precision=lax.Precision.HIGHEST
    )
    y_long = (
        y_blocks.reshape(tok_rows, head_count, HEADDIM)
        + carried
        + d_skip[None, :, None] * x_act.reshape(tok_rows, head_count, HEADDIM).astype(jnp.float32)
    )
    block_states = (jnp.exp(total_log)[:, None, None] * carry_in + local_state)[None]
    normed_long = gate_norm(y_long.reshape(tok_rows, inner_cols), z_long, norm_gain)
    is_valid = jnp.arange(SLEN)[None, :] < lengths[:, None]
    zero_x = jnp.zeros((req_count, rim_rows) + x_short.shape[2:], jnp.bfloat16)
    zero_bc = jnp.zeros((req_count, rim_rows) + bc_short.shape[2:], jnp.bfloat16)
    x_sact = jax.vmap(lambda item: conv_act(item, conv_x, conv_bias_x, SLEN))(
        jnp.concatenate([zero_x, x_short], 1)
    )
    bc_sact = jax.vmap(lambda item: conv_act(item, conv_bc, conv_bias_bc, SLEN))(
        jnp.concatenate([zero_bc, bc_short], 1)
    )
    dt_sfull = jax.nn.softplus(dt_short.astype(jnp.float32) + dt_bias[:, None, None]) * is_valid[
        None
    ].astype(jnp.float32)
    dt_sfull = dt_sfull.transpose(1, 0, 2)

    def per_request(x_req, bc_req, dt_req):
        return ssd_block(
            x_req.reshape(SLEN, head_count, HEADDIM),
            expand(bc_req[:, 0]),
            expand(bc_req[:, 1]),
            dt_req,
            decay_rate,
            start_state,
        )

    y_sblocks, short_states = jax.vmap(per_request)(x_sact, bc_sact, dt_sfull)
    y_short = y_sblocks + d_skip[None, None, :, None] * x_sact.reshape(
        req_count, SLEN, head_count, HEADDIM
    ).astype(jnp.float32)
    normed_short = gate_norm(
        y_short.reshape(req_count * SLEN, inner_cols),
        z_short.reshape(req_count * SLEN, inner_cols),
        norm_gain,
    )
    tail_pick = (
        jnp.arange(SLEN)[None, None, :]
        == (lengths[:, None] - rim_rows + jnp.arange(rim_rows)[None, :])[:, :, None]
    ).astype(jnp.float32)
    tails_x = jnp.einsum(
        "rks,rsc->rkc", tail_pick, x_short.astype(jnp.float32), precision=lax.Precision.HIGHEST
    ).astype(jnp.bfloat16)
    tails_bc = jnp.einsum(
        "rks,rsbc->rkbc", tail_pick, bc_short.astype(jnp.float32), precision=lax.Precision.HIGHEST
    ).astype(jnp.bfloat16)
    all_normed = jnp.concatenate([normed_long, normed_short], 0)
    tp_count = lax.axis_size("tp")
    tp_index = lax.axis_index("tp")
    width = out_weight.shape[1] // tp_count
    total = None
    for step in (2, 1, 3, 0):
        if step >= tp_count:
            continue
        target = (tp_index + step) % tp_count
        piece = lax.dynamic_slice_in_dim(out_weight, target * width, width, 1)
        term = jnp.dot(all_normed, piece, preferred_element_type=jnp.float32).astype(jnp.bfloat16)
        if step:
            route = [(i, (i + step) % tp_count) for i in range(tp_count)]
            half = term.shape[0] // 2
            term = jnp.concatenate(
                [lax.ppermute(term[:half], "tp", route), lax.ppermute(term[half:], "tp", route)], 0
            )
        total = term.astype(jnp.float32) if total is None else total + term.astype(jnp.float32)
    hidden = total.astype(jnp.bfloat16)
    hidden_long = hidden[:tok_rows]
    hidden_short = hidden[tok_rows:].reshape(req_count, SLEN, -1) * is_valid[:, :, None].astype(
        jnp.bfloat16
    )
    last_pick = (jnp.arange(SLEN)[None, :] == lengths[:, None] - 1).astype(jnp.float32)
    short_rows = jnp.einsum(
        "rs,rsd->rd", last_pick, hidden_short.astype(jnp.float32), precision=lax.Precision.HIGHEST
    ).astype(jnp.bfloat16)
    packed = jnp.concatenate([short_rows, hidden_long[tok_rows - 1 :]], 0)
    seq_rows = gather_fast(packed, "seq", 0)
    full_rows = gather_fast(seq_rows, "tp", 1)
    seq_count = lax.axis_size("seq")
    shaped = full_rows.reshape(seq_count, req_count + 1, D)
    long_row = shaped[seq_count - 1, req_count][None]
    short_all = shaped[:, :req_count].reshape(seq_count * req_count, D)
    row_block = jnp.concatenate([long_row, short_all], 0).astype(jnp.float32)
    last_norm = (
        row_block
        * lax.rsqrt(jnp.mean(row_block * row_block, axis=-1, keepdims=True) + 1e-05)
        * final_gain
    ).astype(jnp.bfloat16)
    logits = lax.dot_general(
        last_norm, head_weight, (((1,), (1,)), ((), ())), preferred_element_type=jnp.float32
    )
    top_logit = max_fast(max_fast(jnp.max(logits, axis=1), "tp"), "seq")
    return (
        hidden_long,
        hidden_short,
        block_states,
        short_states,
        tails_x,
        tails_bc,
        last_norm,
        top_logit,
    )


def solution(mesh):
    in_specs = (
        P("seq", "tp"),
        P("seq", None, "tp"),
        P("seq", "tp"),
        P("tp", "seq"),
        P("seq", None, "tp"),
        P("seq", None, None, "tp"),
        P("seq", None, "tp"),
        P("tp", "seq", None),
        P("seq"),
        P(None, "tp"),
        P(None, None, "tp"),
        P("tp"),
        P(None, "tp"),
        P("tp"),
        P("tp"),
        P("tp"),
        P("tp"),
        P("tp", None),
        P(),
        P(("seq", "tp"), None),
    )
    out_specs = (
        P("seq", "tp"),
        P("seq", None, "tp"),
        P("seq", "tp", None, None),
        P("seq", "tp", None, None),
        P("seq", None, "tp"),
        P("seq", None, None, "tp"),
        P(),
        P(),
    )
    return jax.shard_map(local, mesh=mesh, in_specs=in_specs, out_specs=out_specs, check_vma=False)
```

```python
import jax
import jax.numpy as jnp
from jax import lax
from jax.sharding import PartitionSpec as P

D = 4096
HEAD_SHARE = 64
HEADDIM = 64
GROUPS = 4
STATE = 128
KCONV = 4
BLOCK = 256
SLEN = 16


def passed_along(block, axis, distance):
    devices = range(lax.axis_size(axis))
    route = [(i - distance, i) for i in devices if i - distance in devices]
    return lax.ppermute(block, axis, route)


def swapped(block, axis, distance):
    devices = range(lax.axis_size(axis))
    return lax.ppermute(block, axis, [(i, i ^ distance) for i in devices])


def gather_all(block, axis, dim):
    count = lax.axis_size(axis)
    index = lax.axis_index(axis)
    distance = 1
    while distance < count:
        other = swapped(block, axis, distance)
        low = (index // distance) % 2 == 0
        block = jnp.where(
            low, jnp.concatenate([block, other], dim), jnp.concatenate([other, block], dim)
        )
        distance *= 2
    return block


def max_all(block, axis):
    distance = 1
    while distance < lax.axis_size(axis):
        block = jnp.maximum(block, swapped(block, axis, distance))
        distance *= 2
    return block


def digit_route(count, distance, step, radix):
    route = []
    for i in range(count):
        digit = (i // distance) % radix
        route.append((i, i + ((digit + step) % radix - digit) * distance))
    return route


def gather_fast(block, axis, dim):
    count = lax.axis_size(axis)
    index = lax.axis_index(axis)
    distance = 1
    while distance < count:
        radix = min(4, count // distance)
        digit = (index // distance) % radix
        got = [block] + [
            lax.ppermute(block, axis, digit_route(count, distance, step, radix))
            for step in range(1, radix)
        ]
        stacked = jnp.stack(got)
        parts = [
            lax.dynamic_index_in_dim(stacked, (digit - part) % radix, 0, keepdims=False)
            for part in range(radix)
        ]
        block = jnp.concatenate(parts, dim)
        distance *= radix
    return block


def max_fast(block, axis):
    count = lax.axis_size(axis)
    distance = 1
    while distance < count:
        radix = min(4, count // distance)
        got = [
            lax.ppermute(block, axis, digit_route(count, distance, step, radix))
            for step in range(1, radix)
        ]
        for other in got:
            block = jnp.maximum(block, other)
        distance *= radix
    return block


def carry_scan(total_log, local_state, axis):
    sent = local_state.astype(jnp.bfloat16)
    log_one, state_one = passed_along((total_log, sent), axis, 1)
    log_two, state_two = passed_along((total_log, sent), axis, 2)
    seg_log = log_one + log_two
    seg_state = jnp.exp(log_one)[:, None, None] * state_two.astype(jnp.float32) + state_one.astype(
        jnp.float32
    )
    distance = 2
    while distance < lax.axis_size(axis):
        got_log, got_state = passed_along(
            (seg_log, seg_state.astype(jnp.bfloat16)), axis, distance
        )
        seg_state = jnp.exp(seg_log)[:, None, None] * got_state.astype(jnp.float32) + seg_state
        seg_log = seg_log + got_log
        distance *= 2
    return seg_state


def conv_act(padded, weight, shift_bias, span_len):
    running_sum = shift_bias + 0.0 * padded[:span_len].astype(jnp.float32)
    for offset in range(weight.shape[0]):
        running_sum = running_sum + weight[offset] * padded[offset : offset + span_len].astype(
            jnp.float32
        )
    return jax.nn.silu(running_sum).astype(jnp.bfloat16)


def expand(portion):
    shaped = portion.reshape(portion.shape[:-1] + (portion.shape[-1] // STATE, STATE))
    return jnp.repeat(shaped, HEAD_SHARE // GROUPS, axis=-2)


def ssd_block(x_block, b_block, c_block, dt_block, decay_rate, state_in):
    step_log = dt_block * decay_rate[:, None]
    cumulative = jnp.cumsum(step_log, axis=1)
    span_len = x_block.shape[0]
    positions = jnp.arange(span_len)
    causal = (positions[:, None] >= positions[None, :])[None]
    log_gap = jnp.where(causal, cumulative[:, :, None] - cumulative[:, None, :], 0.0)
    decay_table = jnp.where(causal, jnp.exp(log_gap), 0.0)
    scores = jnp.einsum("thn,shn->hts", c_block, b_block, preferred_element_type=jnp.float32)
    weights = (scores * decay_table * dt_block[:, None, :]).astype(jnp.bfloat16)
    y_intra = jnp.einsum("hts,shp->thp", weights, x_block, preferred_element_type=jnp.float32)
    y_state = jnp.exp(cumulative).T[:, :, None] * jnp.einsum(
        "thn,hpn->thp", c_block.astype(jnp.float32), state_in, precision=lax.Precision.HIGHEST
    )
    to_end = jnp.exp(cumulative[:, -1:] - cumulative) * dt_block
    scaled = (x_block.astype(jnp.float32) * to_end.T[:, :, None]).astype(jnp.bfloat16)
    next_state = jnp.exp(cumulative[:, -1])[:, None, None] * state_in + jnp.einsum(
        "shp,shn->hpn", scaled, b_block, preferred_element_type=jnp.float32
    )
    return (y_intra + y_state, next_state)


def gate_norm(values, gating, scales):
    gated_rows = values * jax.nn.silu(gating.astype(jnp.float32))
    size_group = HEAD_SHARE // GROUPS * HEADDIM
    shaped = gated_rows.reshape(gated_rows.shape[0], -1, size_group)
    inv_rms = lax.rsqrt(jnp.mean(shaped * shaped, axis=-1, keepdims=True) + 1e-05)
    return ((shaped * inv_rms).reshape(gated_rows.shape) * scales).astype(jnp.bfloat16)


def local(
    x_long,
    bc_long,
    z_long,
    dt_long,
    x_short,
    bc_short,
    z_short,
    dt_short,
    lengths,
    conv_x,
    conv_bc,
    conv_bias_x,
    conv_bias_bc,
    dt_bias,
    a_log,
    d_skip,
    norm_gain,
    out_weight,
    final_gain,
    head_weight,
):
    tok_rows, inner_cols = x_long.shape
    head_count = dt_long.shape[0]
    req_count = lengths.shape[0]
    rim_rows = KCONV - 1
    decay_rate = -jnp.exp(a_log)
    rim_x, rim_bc = passed_along(
        (x_long[tok_rows - rim_rows :], bc_long[tok_rows - rim_rows :]), "seq", 1
    )
    x_act = conv_act(jnp.concatenate([rim_x, x_long], 0), conv_x, conv_bias_x, tok_rows)
    bc_act = conv_act(jnp.concatenate([rim_bc, bc_long], 0), conv_bc, conv_bias_bc, tok_rows)
    dt_full = jax.nn.softplus(dt_long.astype(jnp.float32) + dt_bias[:, None])
    block_count = tok_rows // BLOCK
    x_blocks = x_act.reshape(block_count, BLOCK, head_count, HEADDIM)
    b_blocks = expand(bc_act[:, 0]).reshape(block_count, BLOCK, head_count, STATE)
    c_all = expand(bc_act[:, 1])
    c_blocks = c_all.reshape(block_count, BLOCK, head_count, STATE)
    dt_blocks = dt_full.reshape(head_count, block_count, BLOCK).transpose(1, 0, 2)

    start_state = jnp.zeros((head_count, HEADDIM, STATE), jnp.float32)
    local_state = start_state
    y_parts = []
    for index in range(block_count):
        y_block, local_state = ssd_block(
            x_blocks[index], b_blocks[index], c_blocks[index], dt_blocks[index], decay_rate, local_state
        )
        y_parts.append(y_block)
    y_blocks = jnp.stack(y_parts)
    cum_device = jnp.cumsum(dt_full * decay_rate[:, None], axis=1)
    total_log = cum_device[:, -1]
    carry_in = carry_scan(total_log, local_state, "seq")
    carried = jnp.exp(cum_device).T[:, :, None] * jnp.einsum(
        "thn,hpn->thp", c_all.astype(jnp.float32), carry_in, precision=lax.Precision.HIGHEST
    )
    y_long = (
        y_blocks.reshape(tok_rows, head_count, HEADDIM)
        + carried
        + d_skip[None, :, None] * x_act.reshape(tok_rows, head_count, HEADDIM).astype(jnp.float32)
    )
    block_states = (jnp.exp(total_log)[:, None, None] * carry_in + local_state)[None]
    normed_long = gate_norm(y_long.reshape(tok_rows, inner_cols), z_long, norm_gain)
    is_valid = jnp.arange(SLEN)[None, :] < lengths[:, None]
    zero_x = jnp.zeros((req_count, rim_rows) + x_short.shape[2:], jnp.bfloat16)
    zero_bc = jnp.zeros((req_count, rim_rows) + bc_short.shape[2:], jnp.bfloat16)
    x_sact = jax.vmap(lambda item: conv_act(item, conv_x, conv_bias_x, SLEN))(
        jnp.concatenate([zero_x, x_short], 1)
    )
    bc_sact = jax.vmap(lambda item: conv_act(item, conv_bc, conv_bias_bc, SLEN))(
        jnp.concatenate([zero_bc, bc_short], 1)
    )
    dt_sfull = jax.nn.softplus(dt_short.astype(jnp.float32) + dt_bias[:, None, None]) * is_valid[
        None
    ].astype(jnp.float32)
    dt_sfull = dt_sfull.transpose(1, 0, 2)

    def per_request(x_req, bc_req, dt_req):
        return ssd_block(
            x_req.reshape(SLEN, head_count, HEADDIM),
            expand(bc_req[:, 0]),
            expand(bc_req[:, 1]),
            dt_req,
            decay_rate,
            start_state,
        )

    y_sblocks, short_states = jax.vmap(per_request)(x_sact, bc_sact, dt_sfull)
    y_short = y_sblocks + d_skip[None, None, :, None] * x_sact.reshape(
        req_count, SLEN, head_count, HEADDIM
    ).astype(jnp.float32)
    normed_short = gate_norm(
        y_short.reshape(req_count * SLEN, inner_cols),
        z_short.reshape(req_count * SLEN, inner_cols),
        norm_gain,
    )
    tail_pick = (
        jnp.arange(SLEN)[None, None, :]
        == (lengths[:, None] - rim_rows + jnp.arange(rim_rows)[None, :])[:, :, None]
    ).astype(jnp.float32)
    tails_x = jnp.einsum(
        "rks,rsc->rkc", tail_pick, x_short.astype(jnp.float32), precision=lax.Precision.HIGHEST
    ).astype(jnp.bfloat16)
    tails_bc = jnp.einsum(
        "rks,rsbc->rkbc", tail_pick, bc_short.astype(jnp.float32), precision=lax.Precision.HIGHEST
    ).astype(jnp.bfloat16)
    all_normed = jnp.concatenate([normed_long, normed_short], 0)
    tp_count = lax.axis_size("tp")
    tp_index = lax.axis_index("tp")
    width = out_weight.shape[1] // tp_count
    total = None
    for step in (2, 1, 3, 0):
        if step >= tp_count:
            continue
        target = (tp_index + step) % tp_count
        piece = lax.dynamic_slice_in_dim(out_weight, target * width, width, 1)
        term = jnp.dot(all_normed, piece, preferred_element_type=jnp.float32).astype(jnp.bfloat16)
        if step:
            term = lax.ppermute(
                term, "tp", [(i, (i + step) % tp_count) for i in range(tp_count)]
            )
        total = term.astype(jnp.float32) if total is None else total + term.astype(jnp.float32)
    hidden = total.astype(jnp.bfloat16)
    hidden_long = hidden[:tok_rows]
    hidden_short = hidden[tok_rows:].reshape(req_count, SLEN, -1) * is_valid[:, :, None].astype(
        jnp.bfloat16
    )
    last_pick = (jnp.arange(SLEN)[None, :] == lengths[:, None] - 1).astype(jnp.float32)
    short_rows = jnp.einsum(
        "rs,rsd->rd", last_pick, hidden_short.astype(jnp.float32), precision=lax.Precision.HIGHEST
    ).astype(jnp.bfloat16)
    packed = jnp.concatenate([short_rows, hidden_long[tok_rows - 1 :]], 0)
    seq_rows = gather_fast(packed, "seq", 0)
    seq_count = lax.axis_size("seq")
    shaped = seq_rows.reshape(seq_count, req_count + 1, -1)
    long_row = shaped[seq_count - 1, req_count][None]
    short_all = shaped[:, :req_count].reshape(seq_count * req_count, -1)
    needed = jnp.concatenate([long_row, short_all], 0)
    row_block = gather_fast(needed, "tp", 1).astype(jnp.float32)
    last_norm = (
        row_block
        * lax.rsqrt(jnp.mean(row_block * row_block, axis=-1, keepdims=True) + 1e-05)
        * final_gain
    ).astype(jnp.bfloat16)
    logits = lax.dot_general(
        last_norm, head_weight, (((1,), (1,)), ((), ())), preferred_element_type=jnp.float32
    )
    top_logit = max_fast(max_fast(jnp.max(logits, axis=1), "tp"), "seq")
    return (
        hidden_long,
        hidden_short,
        block_states,
        short_states,
        tails_x,
        tails_bc,
        last_norm,
        top_logit,
    )


def solution(mesh):
    in_specs = (
        P("seq", "tp"),
        P("seq", None, "tp"),
        P("seq", "tp"),
        P("tp", "seq"),
        P("seq", None, "tp"),
        P("seq", None, None, "tp"),
        P("seq", None, "tp"),
        P("tp", "seq", None),
        P("seq"),
        P(None, "tp"),
        P(None, None, "tp"),
        P("tp"),
        P(None, "tp"),
        P("tp"),
        P("tp"),
        P("tp"),
        P("tp"),
        P("tp", None),
        P(),
        P(("seq", "tp"), None),
    )
    out_specs = (
        P("seq", "tp"),
        P("seq", None, "tp"),
        P("seq", "tp", None, None),
        P("seq", "tp", None, None),
        P("seq", None, "tp"),
        P("seq", None, None, "tp"),
        P(),
        P(),
    )
    return jax.shard_map(local, mesh=mesh, in_specs=in_specs, out_specs=out_specs, check_vma=False)
```

```python
import jax
import jax.numpy as jnp
from jax import lax
from jax.sharding import PartitionSpec as P

D = 4096
HEAD_SHARE = 64
HEADDIM = 64
GROUPS = 4
STATE = 128
KCONV = 4
BLOCK = 256
SLEN = 16


def passed_along(block, axis, distance):
    devices = range(lax.axis_size(axis))
    route = [(i - distance, i) for i in devices if i - distance in devices]
    return lax.ppermute(block, axis, route)


def swapped(block, axis, distance):
    devices = range(lax.axis_size(axis))
    return lax.ppermute(block, axis, [(i, i ^ distance) for i in devices])


def gather_all(block, axis, dim):
    count = lax.axis_size(axis)
    index = lax.axis_index(axis)
    distance = 1
    while distance < count:
        other = swapped(block, axis, distance)
        low = (index // distance) % 2 == 0
        block = jnp.where(
            low, jnp.concatenate([block, other], dim), jnp.concatenate([other, block], dim)
        )
        distance *= 2
    return block


def max_all(block, axis):
    distance = 1
    while distance < lax.axis_size(axis):
        block = jnp.maximum(block, swapped(block, axis, distance))
        distance *= 2
    return block


def digit_route(count, distance, step, radix):
    route = []
    for i in range(count):
        digit = (i // distance) % radix
        route.append((i, i + ((digit + step) % radix - digit) * distance))
    return route


def gather_fast(block, axis, dim):
    count = lax.axis_size(axis)
    index = lax.axis_index(axis)
    distance = 1
    while distance < count:
        radix = min(4, count // distance)
        digit = (index // distance) % radix
        got = [block] + [
            lax.ppermute(block, axis, digit_route(count, distance, step, radix))
            for step in range(1, radix)
        ]
        stacked = jnp.stack(got)
        parts = [
            lax.dynamic_index_in_dim(stacked, (digit - part) % radix, 0, keepdims=False)
            for part in range(radix)
        ]
        block = jnp.concatenate(parts, dim)
        distance *= radix
    return block


def max_fast(block, axis):
    count = lax.axis_size(axis)
    distance = 1
    while distance < count:
        radix = min(4, count // distance)
        got = [
            lax.ppermute(block, axis, digit_route(count, distance, step, radix))
            for step in range(1, radix)
        ]
        for other in got:
            block = jnp.maximum(block, other)
        distance *= radix
    return block


def carry_scan(total_log, local_state, axis):
    sent = local_state.astype(jnp.bfloat16)
    log_one, state_one = passed_along((total_log, sent), axis, 1)
    log_two, state_two = passed_along((total_log, sent), axis, 2)
    seg_log = log_one + log_two
    seg_state = jnp.exp(log_one)[:, None, None] * state_two.astype(jnp.float32) + state_one.astype(
        jnp.float32
    )
    distance = 2
    while distance < lax.axis_size(axis):
        got_log, got_state = passed_along(
            (seg_log, seg_state.astype(jnp.bfloat16)), axis, distance
        )
        seg_state = jnp.exp(seg_log)[:, None, None] * got_state.astype(jnp.float32) + seg_state
        seg_log = seg_log + got_log
        distance *= 2
    return seg_state


def conv_act(padded, weight, shift_bias, span_len):
    running_sum = shift_bias + 0.0 * padded[:span_len].astype(jnp.float32)
    for offset in range(weight.shape[0]):
        running_sum = running_sum + weight[offset] * padded[offset : offset + span_len].astype(
            jnp.float32
        )
    return jax.nn.silu(running_sum).astype(jnp.bfloat16)


def expand(portion):
    shaped = portion.reshape(portion.shape[:-1] + (portion.shape[-1] // STATE, STATE))
    return jnp.repeat(shaped, HEAD_SHARE // GROUPS, axis=-2)


def ssd_block(x_block, b_block, c_block, dt_block, decay_rate, state_in):
    step_log = dt_block * decay_rate[:, None]
    cumulative = jnp.cumsum(step_log, axis=1)
    span_len = x_block.shape[0]
    positions = jnp.arange(span_len)
    causal = (positions[:, None] >= positions[None, :])[None]
    log_gap = jnp.where(causal, cumulative[:, :, None] - cumulative[:, None, :], 0.0)
    decay_table = jnp.where(causal, jnp.exp(log_gap), 0.0)
    scores = jnp.einsum("thn,shn->hts", c_block, b_block, preferred_element_type=jnp.float32)
    weights = (scores * decay_table * dt_block[:, None, :]).astype(jnp.bfloat16)
    y_intra = jnp.einsum("hts,shp->thp", weights, x_block, preferred_element_type=jnp.float32)
    y_state = jnp.exp(cumulative).T[:, :, None] * jnp.einsum(
        "thn,hpn->thp", c_block.astype(jnp.float32), state_in, precision=lax.Precision.HIGHEST
    )
    to_end = jnp.exp(cumulative[:, -1:] - cumulative) * dt_block
    scaled = (x_block.astype(jnp.float32) * to_end.T[:, :, None]).astype(jnp.bfloat16)
    next_state = jnp.exp(cumulative[:, -1])[:, None, None] * state_in + jnp.einsum(
        "shp,shn->hpn", scaled, b_block, preferred_element_type=jnp.float32
    )
    return (y_intra + y_state, next_state)


def gate_norm(values, gating, scales):
    gated_rows = values * jax.nn.silu(gating.astype(jnp.float32))
    size_group = HEAD_SHARE // GROUPS * HEADDIM
    shaped = gated_rows.reshape(gated_rows.shape[0], -1, size_group)
    inv_rms = lax.rsqrt(jnp.mean(shaped * shaped, axis=-1, keepdims=True) + 1e-05)
    return ((shaped * inv_rms).reshape(gated_rows.shape) * scales).astype(jnp.bfloat16)


def local(
    x_long,
    bc_long,
    z_long,
    dt_long,
    x_short,
    bc_short,
    z_short,
    dt_short,
    lengths,
    conv_x,
    conv_bc,
    conv_bias_x,
    conv_bias_bc,
    dt_bias,
    a_log,
    d_skip,
    norm_gain,
    out_weight,
    final_gain,
    head_weight,
):
    tok_rows, inner_cols = x_long.shape
    head_count = dt_long.shape[0]
    req_count = lengths.shape[0]
    rim_rows = KCONV - 1
    decay_rate = -jnp.exp(a_log)
    rim_x, rim_bc = passed_along(
        (x_long[tok_rows - rim_rows :], bc_long[tok_rows - rim_rows :]), "seq", 1
    )
    x_act = conv_act(jnp.concatenate([rim_x, x_long], 0), conv_x, conv_bias_x, tok_rows)
    bc_act = conv_act(jnp.concatenate([rim_bc, bc_long], 0), conv_bc, conv_bias_bc, tok_rows)
    dt_full = jax.nn.softplus(dt_long.astype(jnp.float32) + dt_bias[:, None])
    block_count = tok_rows // BLOCK
    x_blocks = x_act.reshape(block_count, BLOCK, head_count, HEADDIM)
    b_blocks = expand(bc_act[:, 0]).reshape(block_count, BLOCK, head_count, STATE)
    c_all = expand(bc_act[:, 1])
    c_blocks = c_all.reshape(block_count, BLOCK, head_count, STATE)
    dt_blocks = dt_full.reshape(head_count, block_count, BLOCK).transpose(1, 0, 2)

    start_state = jnp.zeros((head_count, HEADDIM, STATE), jnp.float32)
    local_state = start_state
    y_parts = []
    for index in range(block_count):
        y_block, local_state = ssd_block(
            x_blocks[index], b_blocks[index], c_blocks[index], dt_blocks[index], decay_rate, local_state
        )
        y_parts.append(y_block)
    y_blocks = jnp.stack(y_parts)
    cum_device = jnp.cumsum(dt_full * decay_rate[:, None], axis=1)
    total_log = cum_device[:, -1]
    carry_in = carry_scan(total_log, local_state, "seq")
    carried = jnp.exp(cum_device).T[:, :, None] * jnp.einsum(
        "thn,hpn->thp", c_all.astype(jnp.float32), carry_in, precision=lax.Precision.HIGHEST
    )
    y_long = (
        y_blocks.reshape(tok_rows, head_count, HEADDIM)
        + carried
        + d_skip[None, :, None] * x_act.reshape(tok_rows, head_count, HEADDIM).astype(jnp.float32)
    )
    block_states = (jnp.exp(total_log)[:, None, None] * carry_in + local_state)[None]
    normed_long = gate_norm(y_long.reshape(tok_rows, inner_cols), z_long, norm_gain)
    is_valid = jnp.arange(SLEN)[None, :] < lengths[:, None]
    zero_x = jnp.zeros((req_count, rim_rows) + x_short.shape[2:], jnp.bfloat16)
    zero_bc = jnp.zeros((req_count, rim_rows) + bc_short.shape[2:], jnp.bfloat16)
    x_sact = jax.vmap(lambda item: conv_act(item, conv_x, conv_bias_x, SLEN))(
        jnp.concatenate([zero_x, x_short], 1)
    )
    bc_sact = jax.vmap(lambda item: conv_act(item, conv_bc, conv_bias_bc, SLEN))(
        jnp.concatenate([zero_bc, bc_short], 1)
    )
    dt_sfull = jax.nn.softplus(dt_short.astype(jnp.float32) + dt_bias[:, None, None]) * is_valid[
        None
    ].astype(jnp.float32)
    dt_sfull = dt_sfull.transpose(1, 0, 2)

    def per_request(x_req, bc_req, dt_req):
        return ssd_block(
            x_req.reshape(SLEN, head_count, HEADDIM),
            expand(bc_req[:, 0]),
            expand(bc_req[:, 1]),
            dt_req,
            decay_rate,
            start_state,
        )

    y_sblocks, short_states = jax.vmap(per_request)(x_sact, bc_sact, dt_sfull)
    y_short = y_sblocks + d_skip[None, None, :, None] * x_sact.reshape(
        req_count, SLEN, head_count, HEADDIM
    ).astype(jnp.float32)
    normed_short = gate_norm(
        y_short.reshape(req_count * SLEN, inner_cols),
        z_short.reshape(req_count * SLEN, inner_cols),
        norm_gain,
    )
    tail_pick = (
        jnp.arange(SLEN)[None, None, :]
        == (lengths[:, None] - rim_rows + jnp.arange(rim_rows)[None, :])[:, :, None]
    ).astype(jnp.float32)
    tails_x = jnp.einsum(
        "rks,rsc->rkc", tail_pick, x_short.astype(jnp.float32), precision=lax.Precision.HIGHEST
    ).astype(jnp.bfloat16)
    tails_bc = jnp.einsum(
        "rks,rsbc->rkbc", tail_pick, bc_short.astype(jnp.float32), precision=lax.Precision.HIGHEST
    ).astype(jnp.bfloat16)
    all_normed = jnp.concatenate([normed_long, normed_short], 0)
    tp_count = lax.axis_size("tp")
    tp_index = lax.axis_index("tp")
    width = out_weight.shape[1] // tp_count
    last_pick = (jnp.arange(SLEN)[None, :] == lengths[:, None] - 1).astype(jnp.float32)
    total = None
    row_total = None
    for step in (2, 1, 3, 0):
        if step >= tp_count:
            continue
        target = (tp_index + step) % tp_count
        piece = lax.dynamic_slice_in_dim(out_weight, target * width, width, 1)
        term = jnp.dot(all_normed, piece, preferred_element_type=jnp.float32).astype(jnp.bfloat16)
        if step:
            term = lax.ppermute(
                term, "tp", [(i, (i + step) % tp_count) for i in range(tp_count)]
            )
        picked = jnp.concatenate(
            [
                jnp.einsum(
                    "rs,rsd->rd",
                    last_pick,
                    term[tok_rows:].reshape(req_count, SLEN, -1).astype(jnp.float32),
                    precision=lax.Precision.HIGHEST,
                ),
                term[tok_rows - 1 : tok_rows].astype(jnp.float32),
            ],
            0,
        )
        row_total = picked if total is None else row_total + picked
        total = term.astype(jnp.float32) if total is None else total + term.astype(jnp.float32)
    hidden = total.astype(jnp.bfloat16)
    packed = row_total.astype(jnp.bfloat16)
    hidden_long = hidden[:tok_rows]
    hidden_short = hidden[tok_rows:].reshape(req_count, SLEN, -1) * is_valid[:, :, None].astype(
        jnp.bfloat16
    )
    seq_rows = gather_fast(packed, "seq", 0)
    seq_count = lax.axis_size("seq")
    shaped = seq_rows.reshape(seq_count, req_count + 1, -1)
    long_row = shaped[seq_count - 1, req_count][None]
    short_all = shaped[:, :req_count].reshape(seq_count * req_count, -1)
    needed = jnp.concatenate([long_row, short_all], 0)
    row_block = gather_fast(needed, "tp", 1).astype(jnp.float32)
    last_norm = (
        row_block
        * lax.rsqrt(jnp.mean(row_block * row_block, axis=-1, keepdims=True) + 1e-05)
        * final_gain
    ).astype(jnp.bfloat16)
    logits = lax.dot_general(
        last_norm, head_weight, (((1,), (1,)), ((), ())), preferred_element_type=jnp.float32
    )
    top_logit = max_fast(max_fast(jnp.max(logits, axis=1), "tp"), "seq")
    return (
        hidden_long,
        hidden_short,
        block_states,
        short_states,
        tails_x,
        tails_bc,
        last_norm,
        top_logit,
    )


def solution(mesh):
    in_specs = (
        P("seq", "tp"),
        P("seq", None, "tp"),
        P("seq", "tp"),
        P("tp", "seq"),
        P("seq", None, "tp"),
        P("seq", None, None, "tp"),
        P("seq", None, "tp"),
        P("tp", "seq", None),
        P("seq"),
        P(None, "tp"),
        P(None, None, "tp"),
        P("tp"),
        P(None, "tp"),
        P("tp"),
        P("tp"),
        P("tp"),
        P("tp"),
        P("tp", None),
        P(),
        P(("seq", "tp"), None),
    )
    out_specs = (
        P("seq", "tp"),
        P("seq", None, "tp"),
        P("seq", "tp", None, None),
        P("seq", "tp", None, None),
        P("seq", None, "tp"),
        P("seq", None, None, "tp"),
        P(),
        P(),
    )
    return jax.shard_map(local, mesh=mesh, in_specs=in_specs, out_specs=out_specs, check_vma=False)
```
